32 devices in a mesh: rep: 2 (over x), own: 16 (over z, y, core).
Axes of the slice: x: 2, y: 2, z: 4, core: 2. Of those that a mesh axis runs over, the one named last changes fastest.
Arguments:
- gradient: bfloat16 [2, 64, 64, 1024], P('rep', 'own'), may hold values from -6 to 6
- feedback: float32 [2, 64, 64, 1024], P('rep', 'own'), may hold values from -4 to 4
- momentum: float32 [64, 64, 1024], P('own'), may hold values from -6 to 6
- tile_matrix: int32 [64], P('own'), may hold values from 0 to 8, as said below
- matrix_group: int32 [9], replicated, may hold values from 0 to 3
- group_scale: float32 [4], replicated, may hold values from 0.3 to 3
- start_basis: float32 [9, 1024, 32], replicated, may hold values from -0.1875 to 0.1875
- inverse_gram_factors: float32 [3, 9, 32, 32], replicated
- vector_grad: float32 [2, 5, 1024], P('rep'), may hold values from -6 to 6
- vector_momentum: float32 [5, 1024], replicated, may hold values from -6 to 6
Outputs:
- new_feedback: float32 [2, 64, 64, 1024], P('rep', 'own')
- new_momentum: float32 [64, 64, 1024], P('own')
- new_vector_momentum: float32 [5, 1024], replicated
The draws below stay inside these ranges and needn't reach their ends.
Inputs may be any that keep to these rules, and one draw needn't show every extreme that they name: `tile_matrix`: matrices 4 l, 4 l + 1, 4 l + 2, 4 l + 3 are layer l's query, keys, gate and output, matrix 9 - 1 the embedding; with weights 8, 2, 2, 2 per layer and 16 for the embedding, matrix m holds 64 * weight // 44 tiles, and the embedding also takes the tiles left over; the tiles of a matrix lie at scattered positions.
All inputs are finite; a program needn't handle non-finite values.
Results may differ from the reference program's by a relative error of at most 0.0003.
Values sent between devices are 32-bit elements; how exact they have to be, the bound alone decides.
No kernel may reach another device: no remote copies, remote signals or barrier semaphores. Data moves between devices by JAX's collectives and lax.ppermute only.
A program may use at most 64 MiB of HBM per device.

```python
import math
import jax
import jax.numpy as jnp
from jax import lax

D = 1024
R = 32
LAYERS = 2
NGROUP = 4
ROWS_PER_TILE = 64
NMAT = 9
NVEC = 5
REPS = 2
TILES = 64
UNITS = 44


def matrix_tile_counts():
    weights = [8, 2, 2, 2] * LAYERS + [16]
    counts = [TILES * weight // UNITS for weight in weights]
    counts[-1] = counts[-1] + TILES - sum(counts)
    return counts


def draw_tile_matrix(key, part):
    counts = matrix_tile_counts()
    labels = []
    for index in range(NMAT):
        labels = labels + [index] * counts[index]
    order = jax.random.permutation(key, TILES)
    return jnp.asarray(labels, dtype=jnp.int32)[order]


def draw_inverse_gram_factors(key, part):
    first_key = jax.random.fold_in(key, 11)
    second_key = jax.random.fold_in(key, 23)
    counts = matrix_tile_counts()
    row_total = [float(count * ROWS_PER_TILE) for count in counts]
    table = [[1.0] * NMAT, [1.0 / math.sqrt(value) for value in row_total], [1.0 / math.sqrt(D * math.sqrt(R * value)) for value in row_total]]
    factors = jnp.asarray(table, dtype=jnp.float32)
    identity = jnp.eye(R, dtype=jnp.float32)
    main_diagonal = 1.0 + jax.random.uniform(first_key, (3, NMAT, R), jnp.float32)
    spread = jax.random.uniform(second_key, (3, NMAT, R, R), jnp.float32, -0.1, 0.1)
    matrices = identity * main_diagonal[..., None] + spread * (1.0 - identity)
    return matrices * factors[:, :, None, None]


def place_ends(entries, stream_key, low, top_value):
    place = [jax.random.randint(jax.random.fold_in(stream_key, axis), (), 0, length) for axis, length in enumerate(entries.shape)]
    main_axis = entries.shape.index(max(entries.shape))
    next_to = place[:main_axis] + [(place[main_axis] + 1) % entries.shape[main_axis]] + place[main_axis + 1:]
    return entries.at[tuple(place)].set(low).at[tuple(next_to)].set(top_value)


def steps_of(rng, dims, cuts, smallest, top_value):
    level, own = 1.0, jax.random.fold_in(rng, 6)
    for dim, parts in cuts:
        steps = jnp.exp(jax.random.uniform(jax.random.fold_in(own, dim), (parts,), jnp.float32, smallest / len(cuts), top_value / len(cuts)))
        level = level * jnp.repeat(steps, dims[dim] // parts).reshape([-1 if axis == dim else 1 for axis in range(len(dims))])
    return level


def normal_values(rng, extent, deviation, limit, split=(), held_as=jnp.bfloat16):
    factor_of = steps_of(rng, extent, split, -0.22, 0.18) if split else 1.0
    drawn = jax.random.normal(rng, extent, jnp.float32) * deviation * factor_of
    return jnp.minimum(jnp.maximum(drawn, -limit), limit).astype(held_as)


def setup_inputs(seed: int = 0) -> dict:
    key_list = jax.random.split(jax.random.key(seed), 11)
    gradient = normal_values(key_list[0], (REPS, TILES, ROWS_PER_TILE, D), 1.0, 6.0, ((0, 2), (1, 16)))
    feedback = normal_values(key_list[1], (REPS, TILES, ROWS_PER_TILE, D), 0.5, 4.0, ((0, 2), (1, 16)), jnp.float32)
    momentum = normal_values(key_list[2], (TILES, ROWS_PER_TILE, D), 1.0, 6.0, ((0, 16),), jnp.float32)
    tile_matrix = draw_tile_matrix(jax.random.fold_in(key_list[10], 71), 0)
    matrix_group = place_ends(jax.random.randint(key_list[4], (NMAT,), 0, NGROUP), jax.random.fold_in(key_list[4], 1), 0, NGROUP - 1).astype(jnp.int32)
    group_scale = jnp.clip(jnp.exp(jax.random.uniform(key_list[5], (NGROUP,), jnp.float32, math.log(0.3), math.log(3.0))), 0.3, 3.0)
    start_basis = normal_values(key_list[6], (NMAT, D, R), D ** -0.5, 0.1875, (), jnp.float32)
    inverse_gram_factors = draw_inverse_gram_factors(jax.random.fold_in(key_list[10], 71), 0)
    vector_grad = normal_values(key_list[8], (REPS, NVEC, D), 1.0, 6.0, ((0, 2),), jnp.float32)
    vector_momentum = normal_values(key_list[9], (NVEC, D), 1.0, 6.0, (), jnp.float32)
    return dict(gradient=gradient, feedback=feedback, momentum=momentum, tile_matrix=tile_matrix, matrix_group=matrix_group, group_scale=group_scale, start_basis=start_basis, inverse_gram_factors=inverse_gram_factors, vector_grad=vector_grad, vector_momentum=vector_momentum)


TOP_PRECISION = lax.Precision.HIGHEST


def reference(gradient, feedback, momentum, tile_matrix, matrix_group, group_scale, start_basis, inverse_gram_factors, vector_grad, vector_momentum):
    replicas = gradient.shape[0]
    matrix_count = start_basis.shape[0]
    selector = (tile_matrix[:, None] == jnp.arange(matrix_count, dtype=jnp.int32)[None, :]).astype(jnp.float32)
    combined = gradient.astype(jnp.float32) + feedback
    q_tiles = jnp.einsum('tm,mds->tds', selector, start_basis, precision=TOP_PRECISION)
    first_left = jnp.einsum('rtkd,tds->tks', combined, q_tiles, precision=TOP_PRECISION) / replicas
    mix_first = jnp.einsum('tm,mab->tab', selector, inverse_gram_factors[0], precision=TOP_PRECISION)
    first_ortho = jnp.einsum('tks,tsa->tka', first_left, mix_first, precision=TOP_PRECISION)
    first_parts = jnp.einsum('rtkd,tks->tds', combined, first_ortho, precision=TOP_PRECISION)
    initial_table_slice = jnp.einsum('tm,tds->mds', selector, first_parts, precision=TOP_PRECISION) / replicas
    initial_right_factor = jnp.einsum('ltj,ljw->ltw', initial_table_slice, inverse_gram_factors[1], precision=TOP_PRECISION)
    right_tiles = jnp.einsum('tm,mds->tds', selector, initial_right_factor, precision=TOP_PRECISION)
    second_left = jnp.einsum('rtkd,tds->tks', combined, right_tiles, precision=TOP_PRECISION) / replicas
    mix_second = jnp.einsum('tm,mab->tab', selector, inverse_gram_factors[2], precision=TOP_PRECISION)
    second_ortho = jnp.einsum('tks,tsa->tka', second_left, mix_second, precision=TOP_PRECISION)
    second_parts = jnp.einsum('rtkd,tks->tds', combined, second_ortho, precision=TOP_PRECISION)
    second_right = jnp.einsum('tm,tds->mds', selector, second_parts, precision=TOP_PRECISION) / replicas
    back_tiles = jnp.einsum('tm,mds->tds', selector, second_right, precision=TOP_PRECISION)
    approximation = jnp.einsum('tks,tds->tkd', second_ortho, back_tiles, precision=TOP_PRECISION)
    new_feedback = combined - approximation[None]
    group_select = (matrix_group[:, None] == jnp.arange(group_scale.shape[0], dtype=jnp.int32)[None, :]).astype(jnp.float32)
    matrix_scale = jnp.dot(group_select, group_scale, precision=TOP_PRECISION)
    tile_scale = jnp.dot(selector, matrix_scale, precision=TOP_PRECISION)
    new_momentum = 0.9 * momentum + tile_scale[:, None, None] * approximation
    new_vector_momentum = 0.9 * vector_momentum + jnp.sum(vector_grad, axis=0) / replicas
    return (new_feedback, new_momentum, new_vector_momentum)
```

```python
import jax
import jax.numpy as jnp
from jax import lax
from jax.sharding import PartitionSpec as P

TOP_PRECISION = lax.Precision.HIGHEST


def _bits(n):
    return (n - 1).bit_length()


def _pair_perm(n, j):
    return [(i, i ^ (1 << j)) for i in range(n)]


def swap_sum(x, axis):
    n = lax.axis_size(axis)
    for j in range(_bits(n)):
        x = x + lax.ppermute(x, axis, _pair_perm(n, j))
    return x


def _split_plan(shape, steps):
    dims = list(shape)
    plan = []
    for _ in range(steps):
        if dims[-1] > 128:
            axis = len(dims) - 1
        elif dims[-2] > 8:
            axis = len(dims) - 2
        elif dims[-1] % 2 == 0 and dims[-1] >= dims[-2]:
            axis = len(dims) - 1
        else:
            axis = len(dims) - 2
        assert dims[axis] % 2 == 0
        dims[axis] //= 2
        plan.append(axis)
    return plan


def table_sum(x, order):
    steps = []
    for name in order:
        n = lax.axis_size(name)
        for j in range(_bits(n)):
            steps.append((name, j, n))
    plan = _split_plan(x.shape, len(steps))
    bits = []
    cur = x
    for (name, j, n), axis in zip(steps, plan):
        bit = (lax.axis_index(name) >> j) & 1
        half = cur.shape[axis] // 2
        keep = lax.dynamic_slice_in_dim(cur, bit * half, half, axis)
        send = lax.dynamic_slice_in_dim(cur, (1 - bit) * half, half, axis)
        cur = keep + lax.ppermute(send, name, _pair_perm(n, j))
        bits.append(bit)
    for (name, j, n), axis, bit in reversed(list(zip(steps, plan, bits))):
        other = lax.ppermute(cur, name, _pair_perm(n, j))
        low = jnp.where(bit == 0, cur, other)
        high = jnp.where(bit == 0, other, cur)
        cur = jnp.concatenate([low, high], axis=axis)
    return cur


def local(
    gradient,
    feedback,
    momentum,
    tile_matrix,
    matrix_group,
    group_scale,
    start_basis,
    inverse_gram_factors,
    vector_grad,
    vector_momentum,
):
    replicas = lax.axis_size("rep")
    matrix_count = start_basis.shape[0]
    order = ("own", "rep")
    selector = (tile_matrix[:, None] == jnp.arange(matrix_count, dtype=jnp.int32)[None, :]).astype(
        jnp.float32
    )
    combined = gradient[0].astype(jnp.float32) + feedback[0]
    q_tiles = jnp.take(start_basis, tile_matrix, axis=0)
    first_local = jnp.einsum("tkd,tds->tks", combined, q_tiles, precision=TOP_PRECISION)
    vector_summed = swap_sum(vector_grad[0], "rep")
    first_left = swap_sum(first_local, "rep") / replicas
    mix_first = jnp.take(inverse_gram_factors[0], tile_matrix, axis=0)
    first_ortho = jnp.einsum("tks,tsa->tka", first_left, mix_first, precision=TOP_PRECISION)
    first_parts = jnp.einsum("tkd,tks->tsd", combined, first_ortho, precision=TOP_PRECISION)
    first_table = jnp.einsum("tm,tsd->msd", selector, first_parts, precision=TOP_PRECISION)
    first_table = table_sum(first_table, order) / replicas
    first_rows = jnp.take(first_table, tile_matrix, axis=0)
    mix_right = jnp.take(inverse_gram_factors[1], tile_matrix, axis=0)
    right_rows = jnp.einsum("tjw,tjd->twd", mix_right, first_rows, precision=TOP_PRECISION)
    second_local = jnp.einsum("tkd,tsd->tks", combined, right_rows, precision=TOP_PRECISION)
    second_left = swap_sum(second_local, "rep") / replicas
    mix_second = jnp.take(inverse_gram_factors[2], tile_matrix, axis=0)
    second_ortho = jnp.einsum("tks,tsa->tka", second_left, mix_second, precision=TOP_PRECISION)
    second_parts = jnp.einsum("tkd,tks->tsd", combined, second_ortho, precision=TOP_PRECISION)
    second_table = jnp.einsum("tm,tsd->msd", selector, second_parts, precision=TOP_PRECISION)
    second_table = table_sum(second_table, order) / replicas
    back_rows = jnp.take(second_table, tile_matrix, axis=0)
    approximation = jnp.einsum("tks,tsd->tkd", second_ortho, back_rows, precision=TOP_PRECISION)
    new_feedback = (combined - approximation)[None]
    group_select = (
        matrix_group[:, None] == jnp.arange(group_scale.shape[0], dtype=jnp.int32)[None, :]
    ).astype(jnp.float32)
    matrix_scale = jnp.dot(group_select, group_scale, precision=TOP_PRECISION)
    tile_scale = jnp.dot(selector, matrix_scale, precision=TOP_PRECISION)
    new_momentum = 0.9 * momentum + tile_scale[:, None, None] * approximation
    new_vector_momentum = 0.9 * vector_momentum + vector_summed / replicas
    return (new_feedback, new_momentum, new_vector_momentum)


def solution(mesh):
    placed = (
        P("rep", "own", None, None),
        P("rep", "own", None, None),
        P("own", None, None),
        P("own"),
        P(),
        P(),
        P(),
        P(),
        P("rep", None, None),
        P(),
    )
    return jax.shard_map(
        local,
        mesh=mesh,
        in_specs=placed,
        out_specs=(P("rep", "own", None, None), P("own", None, None), P()),
        check_vma=False,
    )
```

```python
import jax
import jax.numpy as jnp
from jax import lax
from jax.sharding import PartitionSpec as P

TOP_PRECISION = lax.Precision.HIGHEST


def _bits(n):
    return (n - 1).bit_length()


def _pair_perm(n, j):
    return [(i, i ^ (1 << j)) for i in range(n)]


def swap_sum(x, axis):
    n = lax.axis_size(axis)
    for j in range(_bits(n)):
        x = x + lax.ppermute(x, axis, _pair_perm(n, j))
    return x


def _split_plan(shape, steps):
    dims = list(shape)
    plan = []
    for _ in range(steps):
        if dims[-1] > 128:
            axis = len(dims) - 1
        elif dims[-2] > 8:
            axis = len(dims) - 2
        elif dims[-1] % 2 == 0 and dims[-1] >= dims[-2]:
            axis = len(dims) - 1
        else:
            axis = len(dims) - 2
        assert dims[axis] % 2 == 0
        dims[axis] //= 2
        plan.append(axis)
    return plan


def table_sum(x, order):
    steps = []
    for name in order:
        n = lax.axis_size(name)
        for j in range(_bits(n)):
            steps.append((name, j, n))
    plan = _split_plan(x.shape, len(steps))
    bits = []
    cur = x
    for (name, j, n), axis in zip(steps, plan):
        bit = (lax.axis_index(name) >> j) & 1
        half = cur.shape[axis] // 2
        keep = lax.dynamic_slice_in_dim(cur, bit * half, half, axis)
        send = lax.dynamic_slice_in_dim(cur, (1 - bit) * half, half, axis)
        cur = keep + lax.ppermute(send, name, _pair_perm(n, j))
        bits.append(bit)
    for (name, j, n), axis, bit in reversed(list(zip(steps, plan, bits))):
        other = lax.ppermute(cur, name, _pair_perm(n, j))
        low = jnp.where(bit == 0, cur, other)
        high = jnp.where(bit == 0, other, cur)
        cur = jnp.concatenate([low, high], axis=axis)
    return cur


def local(
    gradient,
    feedback,
    momentum,
    tile_matrix,
    matrix_group,
    group_scale,
    start_basis,
    inverse_gram_factors,
    vector_grad,
    vector_momentum,
):
    replicas = lax.axis_size("rep")
    matrix_count = start_basis.shape[0]
    order = ("own",)
    selector = (tile_matrix[:, None] == jnp.arange(matrix_count, dtype=jnp.int32)[None, :]).astype(
        jnp.float32
    )
    combined = gradient[0].astype(jnp.float32) + feedback[0]
    tiles, rows, width = combined.shape
    vector_rows = vector_grad.shape[1]
    carried = jnp.concatenate([combined.reshape(tiles * rows, width), vector_grad[0]], axis=0)
    carried = swap_sum(carried, "rep")
    summed = carried[: tiles * rows].reshape(tiles, rows, width)
    vector_summed = carried[tiles * rows : tiles * rows + vector_rows]
    q_tiles = jnp.take(start_basis, tile_matrix, axis=0)
    first_left = jnp.einsum("tkd,tds->tks", summed, q_tiles, precision=TOP_PRECISION) / replicas
    mix_first = jnp.take(inverse_gram_factors[0], tile_matrix, axis=0)
    first_ortho = jnp.einsum("tks,tsa->tka", first_left, mix_first, precision=TOP_PRECISION)
    first_parts = jnp.einsum("tkd,tks->tsd", summed, first_ortho, precision=TOP_PRECISION)
    first_table = jnp.einsum("tm,tsd->msd", selector, first_parts, precision=TOP_PRECISION)
    first_table = table_sum(first_table, order) / replicas
    first_rows = jnp.take(first_table, tile_matrix, axis=0)
    mix_right = jnp.take(inverse_gram_factors[1], tile_matrix, axis=0)
    right_rows = jnp.einsum("tjw,tjd->twd", mix_right, first_rows, precision=TOP_PRECISION)
    second_left = jnp.einsum("tkd,tsd->tks", summed, right_rows, precision=TOP_PRECISION) / replicas
    mix_second = jnp.take(inverse_gram_factors[2], tile_matrix, axis=0)
    second_ortho = jnp.einsum("tks,tsa->tka", second_left, mix_second, precision=TOP_PRECISION)
    second_parts = jnp.einsum("tkd,tks->tsd", summed, second_ortho, precision=TOP_PRECISION)
    second_table = jnp.einsum("tm,tsd->msd", selector, second_parts, precision=TOP_PRECISION)
    second_table = table_sum(second_table, order) / replicas
    back_rows = jnp.take(second_table, tile_matrix, axis=0)
    approximation = jnp.einsum("tks,tsd->tkd", second_ortho, back_rows, precision=TOP_PRECISION)
    new_feedback = (combined - approximation)[None]
    group_select = (
        matrix_group[:, None] == jnp.arange(group_scale.shape[0], dtype=jnp.int32)[None, :]
    ).astype(jnp.float32)
    matrix_scale = jnp.dot(group_select, group_scale, precision=TOP_PRECISION)
    tile_scale = jnp.dot(selector, matrix_scale, precision=TOP_PRECISION)
    new_momentum = 0.9 * momentum + tile_scale[:, None, None] * approximation
    new_vector_momentum = 0.9 * vector_momentum + vector_summed / replicas
    return (new_feedback, new_momentum, new_vector_momentum)


def solution(mesh):
    placed = (
        P("rep", "own", None, None),
        P("rep", "own", None, None),
        P("own", None, None),
        P("own"),
        P(),
        P(),
        P(),
        P(),
        P("rep", None, None),
        P(),
    )
    return jax.shard_map(
        local,
        mesh=mesh,
        in_specs=placed,
        out_specs=(P("rep", "own", None, None), P("own", None, None), P()),
        check_vma=False,
    )
```

```python
import jax
import jax.numpy as jnp
from jax import lax
from jax.sharding import PartitionSpec as P

TOP_PRECISION = lax.Precision.HIGHEST


def _bits(n):
    return (n - 1).bit_length()


def _pair_perm(n, j):
    return [(i, i ^ (1 << j)) for i in range(n)]


def swap_sum(x, axis):
    n = lax.axis_size(axis)
    for j in range(_bits(n)):
        x = x + lax.ppermute(x, axis, _pair_perm(n, j))
    return x


def _split_plan(shape, steps):
    dims = list(shape)
    plan = []
    for _ in range(steps):
        if dims[-1] > 128:
            axis = len(dims) - 1
        elif dims[-2] > 8:
            axis = len(dims) - 2
        elif dims[-1] % 2 == 0 and dims[-1] >= dims[-2]:
            axis = len(dims) - 1
        else:
            axis = len(dims) - 2
        assert dims[axis] % 2 == 0
        dims[axis] //= 2
        plan.append(axis)
    return plan


def table_sum(x, n_rep, n_own):
    axes = ("rep", "own")
    count = n_rep * n_own
    index = lax.axis_index("rep") * n_own + lax.axis_index("own")
    core = index & 1
    own_bits = _bits(n_own)
    rest = list(range(1, own_bits)) + [own_bits + j for j in range(_bits(n_rep))]
    alt = list(rest)
    for i in range(0, len(alt) - 1, 2):
        alt[i], alt[i + 1] = alt[i + 1], alt[i]
    stages = [(0, 0)] + list(zip(rest, alt))
    tail = min(2, len(rest))
    halving = stages[: len(stages) - tail]
    pairing = stages[len(stages) - tail :]

    def perm_of(p0, p1):
        return [(i, i ^ (1 << (p0 if i % 2 == 0 else p1))) for i in range(count)]

    def bit_of(p0, p1):
        return (index >> jnp.where(core == 0, p0, p1)) & 1

    plan = _split_plan(x.shape, len(halving))
    bits = []
    cur = x
    for (p0, p1), axis in zip(halving, plan):
        bit = bit_of(p0, p1)
        half = cur.shape[axis] // 2
        keep = lax.dynamic_slice_in_dim(cur, bit * half, half, axis)
        send = lax.dynamic_slice_in_dim(cur, (1 - bit) * half, half, axis)
        cur = keep + lax.ppermute(send, axes, perm_of(p0, p1))
        bits.append(bit)
    for p0, p1 in pairing:
        cur = cur + lax.ppermute(cur, axes, perm_of(p0, p1))
    for (p0, p1), axis, bit in reversed(list(zip(halving, plan, bits))):
        other = lax.ppermute(cur, axes, perm_of(p0, p1))
        low = jnp.where(bit == 0, cur, other)
        high = jnp.where(bit == 0, other, cur)
        cur = jnp.concatenate([low, high], axis=axis)
    return cur


def local(
    gradient,
    feedback,
    momentum,
    tile_matrix,
    matrix_group,
    group_scale,
    start_basis,
    inverse_gram_factors,
    vector_grad,
    vector_momentum,
):
    replicas = lax.axis_size("rep")
    n_own = lax.axis_size("own")
    matrix_count = start_basis.shape[0]
    selector = (tile_matrix[:, None] == jnp.arange(matrix_count, dtype=jnp.int32)[None, :]).astype(
        jnp.float32
    )
    combined = gradient[0].astype(jnp.float32) + feedback[0]
    q_tiles = jnp.take(start_basis, tile_matrix, axis=0)
    first_local = jnp.einsum("tkd,tds->tks", combined, q_tiles, precision=TOP_PRECISION)
    left_size = first_local.size
    carried = jnp.concatenate([first_local.reshape(-1), vector_grad[0].reshape(-1)])
    carried = swap_sum(carried, "rep")
    first_left = carried[:left_size].reshape(first_local.shape) / replicas
    vector_summed = carried[left_size:].reshape(vector_grad.shape[1:])
    mix_first = jnp.take(inverse_gram_factors[0], tile_matrix, axis=0)
    first_ortho = jnp.einsum("tks,tsa->tka", first_left, mix_first, precision=TOP_PRECISION)
    first_parts = jnp.einsum("tkd,tks->tsd", combined, first_ortho, precision=TOP_PRECISION)
    first_table = jnp.einsum("tm,tsd->msd", selector, first_parts, precision=TOP_PRECISION)
    first_table = table_sum(first_table, replicas, n_own) / replicas
    first_rows = jnp.take(first_table, tile_matrix, axis=0)
    mix_right = jnp.take(inverse_gram_factors[1], tile_matrix, axis=0)
    right_rows = jnp.einsum("tjw,tjd->twd", mix_right, first_rows, precision=TOP_PRECISION)
    second_local = jnp.einsum("tkd,tsd->tks", combined, right_rows, precision=TOP_PRECISION)
    second_left = swap_sum(second_local, "rep") / replicas
    mix_second = jnp.take(inverse_gram_factors[2], tile_matrix, axis=0)
    second_ortho = jnp.einsum("tks,tsa->tka", second_left, mix_second, precision=TOP_PRECISION)
    second_parts = jnp.einsum("tkd,tks->tsd", combined, second_ortho, precision=TOP_PRECISION)
    second_table = jnp.einsum("tm,tsd->msd", selector, second_parts, precision=TOP_PRECISION)
    second_table = table_sum(second_table, replicas, n_own) / replicas
    back_rows = jnp.take(second_table, tile_matrix, axis=0)
    approximation = jnp.einsum("tks,tsd->tkd", second_ortho, back_rows, precision=TOP_PRECISION)
    new_feedback = (combined - approximation)[None]
    group_select = (
        matrix_group[:, None] == jnp.arange(group_scale.shape[0], dtype=jnp.int32)[None, :]
    ).astype(jnp.float32)
    matrix_scale = jnp.dot(group_select, group_scale, precision=TOP_PRECISION)
    tile_scale = jnp.dot(selector, matrix_scale, precision=TOP_PRECISION)
    new_momentum = 0.9 * momentum + tile_scale[:, None, None] * approximation
    new_vector_momentum = 0.9 * vector_momentum + vector_summed / replicas
    return (new_feedback, new_momentum, new_vector_momentum)


def solution(mesh):
    placed = (
        P("rep", "own", None, None),
        P("rep", "own", None, None),
        P("own", None, None),
        P("own"),
        P(),
        P(),
        P(),
        P(),
        P("rep", None, None),
        P(),
    )
    return jax.shard_map(
        local,
        mesh=mesh,
        in_specs=placed,
        out_specs=(P("rep", "own", None, None), P("own", None, None), P()),
        check_vma=False,
    )
```

```python
import jax
import jax.numpy as jnp
from jax import lax
from jax.sharding import PartitionSpec as P

TOP_PRECISION = lax.Precision.HIGHEST


def _bits(n):
    return (n - 1).bit_length()


def _pair_perm(n, j):
    return [(i, i ^ (1 << j)) for i in range(n)]


def swap_sum(x, axis):
    n = lax.axis_size(axis)
    for j in range(_bits(n)):
        x = x + lax.ppermute(x, axis, _pair_perm(n, j))
    return x


def _split_plan(shape, steps):
    dims = list(shape)
    plan = []
    for _ in range(steps):
        if dims[-1] > 128:
            axis = len(dims) - 1
        elif dims[-2] > 8:
            axis = len(dims) - 2
        elif dims[-1] % 2 == 0 and dims[-1] >= dims[-2]:
            axis = len(dims) - 1
        else:
            axis = len(dims) - 2
        assert dims[axis] % 2 == 0
        dims[axis] //= 2
        plan.append(axis)
    return plan


def table_rows(x, rows, n_rep, n_own):
    axes = ("rep", "own")
    count = n_rep * n_own
    index = lax.axis_index("rep") * n_own + lax.axis_index("own")
    core = index & 1
    own_bits = _bits(n_own)
    rest = list(range(1, own_bits)) + [own_bits + j for j in range(_bits(n_rep))]
    alt = list(rest)
    for i in range(0, len(alt) - 1, 2):
        alt[i], alt[i + 1] = alt[i + 1], alt[i]
    stages = [(0, 0)] + list(zip(rest, alt))
    tail = min(2, len(rest))
    halving = stages[: len(stages) - tail]
    pairing = stages[len(stages) - tail :]

    def perm_of(p0, p1):
        return [(i, i ^ (1 << (p0 if i % 2 == 0 else p1))) for i in range(count)]

    def bit_of(p0, p1):
        return (index >> jnp.where(core == 0, p0, p1)) & 1

    plan = _split_plan(x.shape, len(halving))
    bits = []
    cur = x
    for (p0, p1), axis in zip(halving, plan):
        bit = bit_of(p0, p1)
        half = cur.shape[axis] // 2
        keep = lax.dynamic_slice_in_dim(cur, bit * half, half, axis)
        send = lax.dynamic_slice_in_dim(cur, (1 - bit) * half, half, axis)
        cur = keep + lax.ppermute(send, axes, perm_of(p0, p1))
        bits.append(bit)
    for p0, p1 in pairing:
        cur = cur + lax.ppermute(cur, axes, perm_of(p0, p1))
    steps_back = list(reversed(list(zip(halving, plan, bits))))
    for index_step, ((p0, p1), axis, bit) in enumerate(steps_back):
        other = lax.ppermute(cur, axes, perm_of(p0, p1))
        if index_step == len(steps_back) - 1:
            cur = jnp.take(cur, rows, axis=0)
            other = jnp.take(other, rows, axis=0)
        low = jnp.where(bit == 0, cur, other)
        high = jnp.where(bit == 0, other, cur)
        cur = jnp.concatenate([low, high], axis=axis)
    if not steps_back:
        cur = jnp.take(cur, rows, axis=0)
    return cur


def local(
    gradient,
    feedback,
    momentum,
    tile_matrix,
    matrix_group,
    group_scale,
    start_basis,
    inverse_gram_factors,
    vector_grad,
    vector_momentum,
):
    replicas = lax.axis_size("rep")
    n_own = lax.axis_size("own")
    matrix_count = start_basis.shape[0]
    selector = (tile_matrix[:, None] == jnp.arange(matrix_count, dtype=jnp.int32)[None, :]).astype(
        jnp.float32
    )
    combined = gradient[0].astype(jnp.float32) + feedback[0]
    q_tiles = jnp.take(start_basis, tile_matrix, axis=0)
    first_local = jnp.einsum("tkd,tds->tks", combined, q_tiles, precision=TOP_PRECISION)
    left_size = first_local.size
    carried = jnp.concatenate([first_local.reshape(-1), vector_grad[0].reshape(-1)])
    carried = swap_sum(carried, "rep")
    first_left = carried[:left_size].reshape(first_local.shape) / replicas
    vector_summed = carried[left_size:].reshape(vector_grad.shape[1:])
    mix_first = jnp.take(inverse_gram_factors[0], tile_matrix, axis=0)
    first_ortho = jnp.einsum("tks,tsa->tka", first_left, mix_first, precision=TOP_PRECISION)
    first_parts = jnp.einsum("tkd,tks->tsd", combined, first_ortho, precision=TOP_PRECISION)
    first_table = jnp.einsum("tm,tsd->msd", selector, first_parts, precision=TOP_PRECISION)
    first_rows = table_rows(first_table, tile_matrix, replicas, n_own) / replicas
    mix_right = jnp.take(inverse_gram_factors[1], tile_matrix, axis=0)
    right_rows = jnp.einsum("tjw,tjd->twd", mix_right, first_rows, precision=TOP_PRECISION)
    second_local = jnp.einsum("tkd,tsd->tks", combined, right_rows, precision=TOP_PRECISION)
    second_left = swap_sum(second_local, "rep") / replicas
    mix_second = jnp.take(inverse_gram_factors[2], tile_matrix, axis=0)
    second_ortho = jnp.einsum("tks,tsa->tka", second_left, mix_second, precision=TOP_PRECISION)
    second_parts = jnp.einsum("tkd,tks->tsd", combined, second_ortho, precision=TOP_PRECISION)
    second_table = jnp.einsum("tm,tsd->msd", selector, second_parts, precision=TOP_PRECISION)
    back_rows = table_rows(second_table, tile_matrix, replicas, n_own) / replicas
    approximation = jnp.einsum("tks,tsd->tkd", second_ortho, back_rows, precision=TOP_PRECISION)
    new_feedback = (combined - approximation)[None]
    group_select = (
        matrix_group[:, None] == jnp.arange(group_scale.shape[0], dtype=jnp.int32)[None, :]
    ).astype(jnp.float32)
    matrix_scale = jnp.dot(group_select, group_scale, precision=TOP_PRECISION)
    tile_scale = jnp.dot(selector, matrix_scale, precision=TOP_PRECISION)
    new_momentum = 0.9 * momentum + tile_scale[:, None, None] * approximation
    new_vector_momentum = 0.9 * vector_momentum + vector_summed / replicas
    return (new_feedback, new_momentum, new_vector_momentum)


def solution(mesh):
    placed = (
        P("rep", "own", None, None),
        P("rep", "own", None, None),
        P("own", None, None),
        P("own"),
        P(),
        P(),
        P(),
        P(),
        P("rep", None, None),
        P(),
    )
    return jax.shard_map(
        local,
        mesh=mesh,
        in_specs=placed,
        out_specs=(P("rep", "own", None, None), P("own", None, None), P()),
        check_vma=False,
    )
```

```python
import jax
import jax.numpy as jnp
from jax import lax
from jax.sharding import PartitionSpec as P

TOP_PRECISION = lax.Precision.HIGHEST


def _bits(n):
    return (n - 1).bit_length()


def _pair_perm(n, j):
    return [(i, i ^ (1 << j)) for i in range(n)]


def swap_sum(x, axis):
    n = lax.axis_size(axis)
    for j in range(_bits(n)):
        x = x + lax.ppermute(x, axis, _pair_perm(n, j))
    return x


def _split_plan(shape, steps):
    dims = list(shape)
    plan = []
    for _ in range(steps):
        if dims[-1] > 128:
            axis = len(dims) - 1
        elif dims[-2] > 8:
            axis = len(dims) - 2
        elif dims[-1] % 2 == 0 and dims[-1] >= dims[-2]:
            axis = len(dims) - 1
        else:
            axis = len(dims) - 2
        assert dims[axis] % 2 == 0
        dims[axis] //= 2
        plan.append(axis)
    return plan


def _pick_rows(table, rows):
    return jnp.stack([lax.dynamic_index_in_dim(table, rows[i], 0, keepdims=False) for i in range(rows.shape[0])])


def table_rows(x, rows, n_rep, n_own):
    axes = ("rep", "own")
    count = n_rep * n_own
    index = lax.axis_index("rep") * n_own + lax.axis_index("own")
    core = index & 1
    own_bits = _bits(n_own)
    rest = list(range(1, own_bits)) + [own_bits + j for j in range(_bits(n_rep))]
    alt = list(rest)
    for i in range(0, len(alt) - 1, 2):
        alt[i], alt[i + 1] = alt[i + 1], alt[i]
    stages = [(0, 0)] + list(zip(rest, alt))
    tail = min(2, len(rest))
    halving = stages[: len(stages) - tail]
    pairing = stages[len(stages) - tail :]

    def perm_of(p0, p1):
        return [(i, i ^ (1 << (p0 if i % 2 == 0 else p1))) for i in range(count)]

    def bit_of(p0, p1):
        return (index >> jnp.where(core == 0, p0, p1)) & 1

    plan = _split_plan(x.shape, len(halving))
    bits = []
    cur = x
    for (p0, p1), axis in zip(halving, plan):
        bit = bit_of(p0, p1)
        half = cur.shape[axis] // 2
        keep = lax.dynamic_slice_in_dim(cur, bit * half, half, axis)
        send = lax.dynamic_slice_in_dim(cur, (1 - bit) * half, half, axis)
        cur = keep + lax.ppermute(send, axes, perm_of(p0, p1))
        bits.append(bit)
    for p0, p1 in pairing:
        cur = cur + lax.ppermute(cur, axes, perm_of(p0, p1))
    steps_back = list(reversed(list(zip(halving, plan, bits))))
    for index_step, ((p0, p1), axis, bit) in enumerate(steps_back):
        other = lax.ppermute(cur, axes, perm_of(p0, p1))
        if index_step == len(steps_back) - 1:
            cur = _pick_rows(cur, rows)
            other = _pick_rows(other, rows)
        low = jnp.where(bit == 0, cur, other)
        high = jnp.where(bit == 0, other, cur)
        cur = jnp.concatenate([low, high], axis=axis)
    if not steps_back:
        cur = _pick_rows(cur, rows)
    return cur


def local(
    gradient,
    feedback,
    momentum,
    tile_matrix,
    matrix_group,
    group_scale,
    start_basis,
    inverse_gram_factors,
    vector_grad,
    vector_momentum,
):
    replicas = lax.axis_size("rep")
    n_own = lax.axis_size("own")
    matrix_count = start_basis.shape[0]
    selector = (tile_matrix[:, None] == jnp.arange(matrix_count, dtype=jnp.int32)[None, :]).astype(
        jnp.float32
    )
    combined = gradient[0].astype(jnp.float32) + feedback[0]
    q_tiles = jnp.take(start_basis, tile_matrix, axis=0)
    first_local = jnp.einsum("tkd,tds->tks", combined, q_tiles, precision=TOP_PRECISION)
    left_size = first_local.size
    carried = jnp.concatenate([first_local.reshape(-1), vector_grad[0].reshape(-1)])
    carried = swap_sum(carried, "rep")
    first_left = carried[:left_size].reshape(first_local.shape) / replicas
    vector_summed = carried[left_size:].reshape(vector_grad.shape[1:])
    mix_first = jnp.take(inverse_gram_factors[0], tile_matrix, axis=0)
    first_ortho = jnp.einsum("tks,tsa->tka", first_left, mix_first, precision=TOP_PRECISION)
    first_parts = jnp.einsum("tkd,tks->tsd", combined, first_ortho, precision=TOP_PRECISION)
    first_table = jnp.einsum("tm,tsd->msd", selector, first_parts, precision=TOP_PRECISION)
    first_rows = table_rows(first_table, tile_matrix, replicas, n_own) / replicas
    mix_right = jnp.take(inverse_gram_factors[1], tile_matrix, axis=0)
    right_rows = jnp.einsum("tjw,tjd->twd", mix_right, first_rows, precision=TOP_PRECISION)
    second_local = jnp.einsum("tkd,tsd->tks", combined, right_rows, precision=TOP_PRECISION)
    second_left = swap_sum(second_local, "rep") / replicas
    mix_second = jnp.take(inverse_gram_factors[2], tile_matrix, axis=0)
    second_ortho = jnp.einsum("tks,tsa->tka", second_left, mix_second, precision=TOP_PRECISION)
    second_parts = jnp.einsum("tkd,tks->tsd", combined, second_ortho, precision=TOP_PRECISION)
    second_table = jnp.einsum("tm,tsd->msd", selector, second_parts, precision=TOP_PRECISION)
    back_rows = table_rows(second_table, tile_matrix, replicas, n_own) / replicas
    approximation = jnp.einsum("tks,tsd->tkd", second_ortho, back_rows, precision=TOP_PRECISION)
    new_feedback = (combined - approximation)[None]
    group_select = (
        matrix_group[:, None] == jnp.arange(group_scale.shape[0], dtype=jnp.int32)[None, :]
    ).astype(jnp.float32)
    matrix_scale = jnp.dot(group_select, group_scale, precision=TOP_PRECISION)
    tile_scale = jnp.dot(selector, matrix_scale, precision=TOP_PRECISION)
    new_momentum = 0.9 * momentum + tile_scale[:, None, None] * approximation
    new_vector_momentum = 0.9 * vector_momentum + vector_summed / replicas
    return (new_feedback, new_momentum, new_vector_momentum)


def solution(mesh):
    placed = (
        P("rep", "own", None, None),
        P("rep", "own", None, None),
        P("own", None, None),
        P("own"),
        P(),
        P(),
        P(),
        P(),
        P("rep", None, None),
        P(),
    )
    return jax.shard_map(
        local,
        mesh=mesh,
        in_specs=placed,
        out_specs=(P("rep", "own", None, None), P("own", None, None), P()),
        check_vma=False,
    )
```

```python
import jax
import jax.numpy as jnp
from jax import lax
from jax.sharding import PartitionSpec as P

TOP_PRECISION = lax.Precision.HIGHEST


def _bits(n):
    return (n - 1).bit_length()


def _pair_perm(n, j):
    return [(i, i ^ (1 << j)) for i in range(n)]


def swap_sum(x, axis):
    n = lax.axis_size(axis)
    for j in range(_bits(n)):
        x = x + lax.ppermute(x, axis, _pair_perm(n, j))
    return x


def _split_plan(shape, steps):
    dims = list(shape)
    plan = []
    for _ in range(steps):
        if dims[-1] > 128:
            axis = len(dims) - 1
        elif dims[-2] > 8:
            axis = len(dims) - 2
        elif dims[-1] % 2 == 0 and dims[-1] >= dims[-2]:
            axis = len(dims) - 1
        else:
            axis = len(dims) - 2
        assert dims[axis] % 2 == 0
        dims[axis] //= 2
        plan.append(axis)
    return plan


def _pick_rows(table, rows):
    return jnp.stack([lax.dynamic_index_in_dim(table, rows[i], 0, keepdims=False) for i in range(rows.shape[0])])


def _scatter_rows(parts, rows, count):
    table = jnp.zeros((count,) + parts.shape[1:], parts.dtype)
    for i in range(parts.shape[0]):
        slab = lax.dynamic_index_in_dim(table, rows[i], 0, keepdims=True)
        table = lax.dynamic_update_index_in_dim(table, slab + parts[i : i + 1], rows[i], 0)
    return table


def table_rows(x, rows, n_rep, n_own):
    axes = ("rep", "own")
    count = n_rep * n_own
    index = lax.axis_index("rep") * n_own + lax.axis_index("own")
    core = index & 1
    own_bits = _bits(n_own)
    rest = list(range(1, own_bits)) + [own_bits + j for j in range(_bits(n_rep))]
    alt = list(rest)
    for i in range(0, len(alt) - 1, 2):
        alt[i], alt[i + 1] = alt[i + 1], alt[i]
    stages = [(0, 0)] + list(zip(rest, alt))
    tail = min(2, len(rest))
    halving = stages[: len(stages) - tail]
    pairing = stages[len(stages) - tail :]

    def perm_of(p0, p1):
        return [(i, i ^ (1 << (p0 if i % 2 == 0 else p1))) for i in range(count)]

    def bit_of(p0, p1):
        return (index >> jnp.where(core == 0, p0, p1)) & 1

    plan = _split_plan(x.shape, len(halving))
    bits = []
    cur = x
    for (p0, p1), axis in zip(halving, plan):
        bit = bit_of(p0, p1)
        half = cur.shape[axis] // 2
        keep = lax.dynamic_slice_in_dim(cur, bit * half, half, axis)
        send = lax.dynamic_slice_in_dim(cur, (1 - bit) * half, half, axis)
        cur = keep + lax.ppermute(send, axes, perm_of(p0, p1))
        bits.append(bit)
    for p0, p1 in pairing:
        cur = cur + lax.ppermute(cur, axes, perm_of(p0, p1))
    steps_back = list(reversed(list(zip(halving, plan, bits))))
    for index_step, ((p0, p1), axis, bit) in enumerate(steps_back):
        other = lax.ppermute(cur, axes, perm_of(p0, p1))
        if index_step == len(steps_back) - 1:
            cur = _pick_rows(cur, rows)
            other = _pick_rows(other, rows)
        low = jnp.where(bit == 0, cur, other)
        high = jnp.where(bit == 0, other, cur)
        cur = jnp.concatenate([low, high], axis=axis)
    if not steps_back:
        cur = _pick_rows(cur, rows)
    return cur


def local(
    gradient,
    feedback,
    momentum,
    tile_matrix,
    matrix_group,
    group_scale,
    start_basis,
    inverse_gram_factors,
    vector_grad,
    vector_momentum,
):
    replicas = lax.axis_size("rep")
    n_own = lax.axis_size("own")
    matrix_count = start_basis.shape[0]
    selector = (tile_matrix[:, None] == jnp.arange(matrix_count, dtype=jnp.int32)[None, :]).astype(
        jnp.float32
    )
    combined = gradient[0].astype(jnp.float32) + feedback[0]
    q_tiles = _pick_rows(start_basis, tile_matrix)
    first_local = jnp.einsum("tkd,tds->tks", combined, q_tiles, precision=TOP_PRECISION)
    left_size = first_local.size
    carried = jnp.concatenate([first_local.reshape(-1), vector_grad[0].reshape(-1)])
    carried = swap_sum(carried, "rep")
    first_left = carried[:left_size].reshape(first_local.shape) / replicas
    vector_summed = carried[left_size:].reshape(vector_grad.shape[1:])
    mix_first = _pick_rows(inverse_gram_factors[0], tile_matrix)
    first_ortho = jnp.einsum("tks,tsa->tka", first_left, mix_first, precision=TOP_PRECISION)
    first_parts = jnp.einsum("tkd,tks->tsd", combined, first_ortho, precision=TOP_PRECISION)
    first_table = _scatter_rows(first_parts, tile_matrix, matrix_count)
    first_rows = table_rows(first_table, tile_matrix, replicas, n_own) / replicas
    mix_right = _pick_rows(inverse_gram_factors[1], tile_matrix)
    right_rows = jnp.einsum("tjw,tjd->twd", mix_right, first_rows, precision=TOP_PRECISION)
    second_local = jnp.einsum("tkd,tsd->tks", combined, right_rows, precision=TOP_PRECISION)
    second_left = swap_sum(second_local, "rep") / replicas
    mix_second = _pick_rows(inverse_gram_factors[2], tile_matrix)
    second_ortho = jnp.einsum("tks,tsa->tka", second_left, mix_second, precision=TOP_PRECISION)
    second_parts = jnp.einsum("tkd,tks->tsd", combined, second_ortho, precision=TOP_PRECISION)
    second_table = _scatter_rows(second_parts, tile_matrix, matrix_count)
    back_rows = table_rows(second_table, tile_matrix, replicas, n_own) / replicas
    approximation = jnp.einsum("tks,tsd->tkd", second_ortho, back_rows, precision=TOP_PRECISION)
    new_feedback = (combined - approximation)[None]
    group_select = (
        matrix_group[:, None] == jnp.arange(group_scale.shape[0], dtype=jnp.int32)[None, :]
    ).astype(jnp.float32)
    matrix_scale = jnp.dot(group_select, group_scale, precision=TOP_PRECISION)
    tile_scale = jnp.dot(selector, matrix_scale, precision=TOP_PRECISION)
    new_momentum = 0.9 * momentum + tile_scale[:, None, None] * approximation
    new_vector_momentum = 0.9 * vector_momentum + vector_summed / replicas
    return (new_feedback, new_momentum, new_vector_momentum)


def solution(mesh):
    placed = (
        P("rep", "own", None, None),
        P("rep", "own", None, None),
        P("own", None, None),
        P("own"),
        P(),
        P(),
        P(),
        P(),
        P("rep", None, None),
        P(),
    )
    return jax.shard_map(
        local,
        mesh=mesh,
        in_specs=placed,
        out_specs=(P("rep", "own", None, None), P("own", None, None), P()),
        check_vma=False,
    )
```

```python
import jax
import jax.numpy as jnp
from jax import lax
from jax.sharding import PartitionSpec as P

TOP_PRECISION = lax.Precision.HIGHEST


def _bits(n):
    return (n - 1).bit_length()


def _pair_perm(n, j):
    return [(i, i ^ (1 << j)) for i in range(n)]


def swap_sum(x, axis):
    n = lax.axis_size(axis)
    for j in range(_bits(n)):
        x = x + lax.ppermute(x, axis, _pair_perm(n, j))
    return x


def _split_plan(shape, steps):
    dims = list(shape)
    plan = []
    for _ in range(steps):
        if dims[-1] > 128:
            axis = len(dims) - 1
        elif dims[-2] > 8:
            axis = len(dims) - 2
        elif dims[-1] % 2 == 0 and dims[-1] >= dims[-2]:
            axis = len(dims) - 1
        else:
            axis = len(dims) - 2
        assert dims[axis] % 2 == 0
        dims[axis] //= 2
        plan.append(axis)
    return plan


def _pick_rows(table, rows):
    return jnp.stack([lax.dynamic_index_in_dim(table, rows[i], 0, keepdims=False) for i in range(rows.shape[0])])


def _scatter_rows(parts, rows, count):
    table = jnp.zeros((count,) + parts.shape[1:], parts.dtype)
    for i in range(parts.shape[0]):
        slab = lax.dynamic_index_in_dim(table, rows[i], 0, keepdims=True)
        table = lax.dynamic_update_index_in_dim(table, slab + parts[i : i + 1], rows[i], 0)
    return table


def table_rows(x, rows, n_rep, n_own):
    axes = ("rep", "own")
    count = n_rep * n_own
    index = lax.axis_index("rep") * n_own + lax.axis_index("own")
    core = index & 1
    own_bits = _bits(n_own)
    rest = list(range(1, own_bits)) + [own_bits + j for j in range(_bits(n_rep))]
    alt = list(rest)
    for i in range(0, len(alt) - 1, 2):
        alt[i], alt[i + 1] = alt[i + 1], alt[i]
    stages = [(0, 0)] + list(zip(rest, alt))
    tail = min(2, len(rest))
    halving = stages[: len(stages) - tail]
    pairing = stages[len(stages) - tail :]

    def perm_of(p0, p1):
        return [(i, i ^ (1 << (p0 if i % 2 == 0 else p1))) for i in range(count)]

    def bit_of(p0, p1):
        return (index >> jnp.where(core == 0, p0, p1)) & 1

    plan = _split_plan(x.shape, len(halving))
    bits = []
    cur = x
    for (p0, p1), axis in zip(halving, plan):
        bit = bit_of(p0, p1)
        half = cur.shape[axis] // 2
        keep = lax.dynamic_slice_in_dim(cur, bit * half, half, axis)
        send = lax.dynamic_slice_in_dim(cur, (1 - bit) * half, half, axis)
        cur = keep + lax.ppermute(send, axes, perm_of(p0, p1))
        bits.append(bit)
    for p0, p1 in pairing:
        cur = cur + lax.ppermute(cur, axes, perm_of(p0, p1))
    steps_back = list(reversed(list(zip(halving, plan, bits))))
    for index_step, ((p0, p1), axis, bit) in enumerate(steps_back):
        other = lax.ppermute(cur, axes, perm_of(p0, p1))
        if index_step == len(steps_back) - 1:
            cur = _pick_rows(cur, rows)
            other = _pick_rows(other, rows)
        low = jnp.where(bit == 0, cur, other)
        high = jnp.where(bit == 0, other, cur)
        cur = jnp.concatenate([low, high], axis=axis)
    if not steps_back:
        cur = _pick_rows(cur, rows)
    return cur


def local(
    gradient,
    feedback,
    momentum,
    tile_matrix,
    matrix_group,
    group_scale,
    start_basis,
    inverse_gram_factors,
    vector_grad,
    vector_momentum,
):
    replicas = lax.axis_size("rep")
    n_own = lax.axis_size("own")
    matrix_count = start_basis.shape[0]
    selector = (tile_matrix[:, None] == jnp.arange(matrix_count, dtype=jnp.int32)[None, :]).astype(
        jnp.float32
    )
    combined = gradient[0].astype(jnp.float32) + feedback[0]
    q_tiles = start_basis.at[tile_matrix].get(mode="promise_in_bounds")
    first_local = jnp.einsum("tkd,tds->tks", combined, q_tiles, precision=TOP_PRECISION)
    left_size = first_local.size
    carried = jnp.concatenate([first_local.reshape(-1), vector_grad[0].reshape(-1)])
    carried = swap_sum(carried, "rep")
    first_left = carried[:left_size].reshape(first_local.shape) / replicas
    vector_summed = carried[left_size:].reshape(vector_grad.shape[1:])
    mix_first = inverse_gram_factors[0].at[tile_matrix].get(mode="promise_in_bounds")
    first_ortho = jnp.einsum("tks,tsa->tka", first_left, mix_first, precision=TOP_PRECISION)
    first_parts = jnp.einsum("tkd,tks->tsd", combined, first_ortho, precision=TOP_PRECISION)
    first_table = _scatter_rows(first_parts, tile_matrix, matrix_count)
    first_rows = table_rows(first_table, tile_matrix, replicas, n_own) / replicas
    mix_right = inverse_gram_factors[1].at[tile_matrix].get(mode="promise_in_bounds")
    right_rows = jnp.einsum("tjw,tjd->twd", mix_right, first_rows, precision=TOP_PRECISION)
    second_local = jnp.einsum("tkd,tsd->tks", combined, right_rows, precision=TOP_PRECISION)
    second_left = swap_sum(second_local, "rep") / replicas
    mix_second = inverse_gram_factors[2].at[tile_matrix].get(mode="promise_in_bounds")
    second_ortho = jnp.einsum("tks,tsa->tka", second_left, mix_second, precision=TOP_PRECISION)
    second_parts = jnp.einsum("tkd,tks->tsd", combined, second_ortho, precision=TOP_PRECISION)
    second_table = _scatter_rows(second_parts, tile_matrix, matrix_count)
    back_rows = table_rows(second_table, tile_matrix, replicas, n_own) / replicas
    approximation = jnp.einsum("tks,tsd->tkd", second_ortho, back_rows, precision=TOP_PRECISION)
    new_feedback = (combined - approximation)[None]
    group_select = (
        matrix_group[:, None] == jnp.arange(group_scale.shape[0], dtype=jnp.int32)[None, :]
    ).astype(jnp.float32)
    matrix_scale = jnp.dot(group_select, group_scale, precision=TOP_PRECISION)
    tile_scale = jnp.dot(selector, matrix_scale, precision=TOP_PRECISION)
    new_momentum = 0.9 * momentum + tile_scale[:, None, None] * approximation
    new_vector_momentum = 0.9 * vector_momentum + vector_summed / replicas
    return (new_feedback, new_momentum, new_vector_momentum)


def solution(mesh):
    placed = (
        P("rep", "own", None, None),
        P("rep", "own", None, None),
        P("own", None, None),
        P("own"),
        P(),
        P(),
        P(),
        P(),
        P("rep", None, None),
        P(),
    )
    return jax.shard_map(
        local,
        mesh=mesh,
        in_specs=placed,
        out_specs=(P("rep", "own", None, None), P("own", None, None), P()),
        check_vma=False,
    )
```

```python
import jax
import jax.numpy as jnp
from jax import lax
from jax.sharding import PartitionSpec as P

TOP_PRECISION = lax.Precision.HIGHEST


def _bits(n):
    return (n - 1).bit_length()


def _pair_perm(n, j):
    return [(i, i ^ (1 << j)) for i in range(n)]


def swap_sum(x, axis):
    n = lax.axis_size(axis)
    for j in range(_bits(n)):
        x = x + lax.ppermute(x, axis, _pair_perm(n, j))
    return x


def _split_plan(shape, steps):
    dims = list(shape)
    plan = []
    for _ in range(steps):
        if dims[-1] > 128:
            axis = len(dims) - 1
        elif dims[-2] > 8:
            axis = len(dims) - 2
        elif dims[-1] % 2 == 0 and dims[-1] >= dims[-2]:
            axis = len(dims) - 1
        else:
            axis = len(dims) - 2
        assert dims[axis] % 2 == 0
        dims[axis] //= 2
        plan.append(axis)
    return plan


def _pick_rows(table, rows):
    return jnp.stack([lax.dynamic_index_in_dim(table, rows[i], 0, keepdims=False) for i in range(rows.shape[0])])


def _scatter_rows(parts, rows, count):
    slots = jnp.arange(count, dtype=rows.dtype)[:, None, None]
    table = None
    for i in range(parts.shape[0]):
        term = jnp.where(slots == rows[i], parts[i][None], 0.0)
        table = term if table is None else table + term
    return table


def table_rows(x, rows, n_rep, n_own):
    axes = ("rep", "own")
    count = n_rep * n_own
    index = lax.axis_index("rep") * n_own + lax.axis_index("own")
    core = index & 1
    own_bits = _bits(n_own)
    rest = list(range(1, own_bits)) + [own_bits + j for j in range(_bits(n_rep))]
    alt = list(rest)
    for i in range(0, len(alt) - 1, 2):
        alt[i], alt[i + 1] = alt[i + 1], alt[i]
    stages = [(0, 0)] + list(zip(rest, alt))
    tail = min(2, len(rest))
    halving = stages[: len(stages) - tail]
    pairing = stages[len(stages) - tail :]

    def perm_of(p0, p1):
        return [(i, i ^ (1 << (p0 if i % 2 == 0 else p1))) for i in range(count)]

    def bit_of(p0, p1):
        return (index >> jnp.where(core == 0, p0, p1)) & 1

    plan = _split_plan(x.shape, len(halving))
    bits = []
    cur = x
    for (p0, p1), axis in zip(halving, plan):
        bit = bit_of(p0, p1)
        half = cur.shape[axis] // 2
        keep = lax.dynamic_slice_in_dim(cur, bit * half, half, axis)
        send = lax.dynamic_slice_in_dim(cur, (1 - bit) * half, half, axis)
        cur = keep + lax.ppermute(send, axes, perm_of(p0, p1))
        bits.append(bit)
    for p0, p1 in pairing:
        cur = cur + lax.ppermute(cur, axes, perm_of(p0, p1))
    steps_back = list(reversed(list(zip(halving, plan, bits))))
    for index_step, ((p0, p1), axis, bit) in enumerate(steps_back):
        other = lax.ppermute(cur, axes, perm_of(p0, p1))
        if index_step == len(steps_back) - 1:
            cur = _pick_rows(cur, rows)
            other = _pick_rows(other, rows)
        low = jnp.where(bit == 0, cur, other)
        high = jnp.where(bit == 0, other, cur)
        cur = jnp.concatenate([low, high], axis=axis)
    if not steps_back:
        cur = _pick_rows(cur, rows)
    return cur


def local(
    gradient,
    feedback,
    momentum,
    tile_matrix,
    matrix_group,
    group_scale,
    start_basis,
    inverse_gram_factors,
    vector_grad,
    vector_momentum,
):
    replicas = lax.axis_size("rep")
    n_own = lax.axis_size("own")
    matrix_count = start_basis.shape[0]
    selector = (tile_matrix[:, None] == jnp.arange(matrix_count, dtype=jnp.int32)[None, :]).astype(
        jnp.float32
    )
    combined = gradient[0].astype(jnp.float32) + feedback[0]
    q_tiles = start_basis.at[tile_matrix].get(mode="promise_in_bounds")
    first_local = jnp.einsum("tkd,tds->tks", combined, q_tiles, precision=TOP_PRECISION)
    left_size = first_local.size
    carried = jnp.concatenate([first_local.reshape(-1), vector_grad[0].reshape(-1)])
    carried = swap_sum(carried, "rep")
    first_left = carried[:left_size].reshape(first_local.shape) / replicas
    vector_summed = carried[left_size:].reshape(vector_grad.shape[1:])
    mix_first = inverse_gram_factors[0].at[tile_matrix].get(mode="promise_in_bounds")
    first_ortho = jnp.einsum("tks,tsa->tka", first_left, mix_first, precision=TOP_PRECISION)
    first_parts = jnp.einsum("tkd,tks->tsd", combined, first_ortho, precision=TOP_PRECISION)
    first_table = _scatter_rows(first_parts, tile_matrix, matrix_count)
    first_rows = table_rows(first_table, tile_matrix, replicas, n_own) / replicas
    mix_right = inverse_gram_factors[1].at[tile_matrix].get(mode="promise_in_bounds")
    right_rows = jnp.einsum("tjw,tjd->twd", mix_right, first_rows, precision=TOP_PRECISION)
    second_local = jnp.einsum("tkd,tsd->tks", combined, right_rows, precision=TOP_PRECISION)
    second_left = swap_sum(second_local, "rep") / replicas
    mix_second = inverse_gram_factors[2].at[tile_matrix].get(mode="promise_in_bounds")
    second_ortho = jnp.einsum("tks,tsa->tka", second_left, mix_second, precision=TOP_PRECISION)
    second_parts = jnp.einsum("tkd,tks->tsd", combined, second_ortho, precision=TOP_PRECISION)
    second_table = _scatter_rows(second_parts, tile_matrix, matrix_count)
    back_rows = table_rows(second_table, tile_matrix, replicas, n_own) / replicas
    approximation = jnp.einsum("tks,tsd->tkd", second_ortho, back_rows, precision=TOP_PRECISION)
    new_feedback = (combined - approximation)[None]
    group_select = (
        matrix_group[:, None] == jnp.arange(group_scale.shape[0], dtype=jnp.int32)[None, :]
    ).astype(jnp.float32)
    matrix_scale = jnp.dot(group_select, group_scale, precision=TOP_PRECISION)
    tile_scale = jnp.dot(selector, matrix_scale, precision=TOP_PRECISION)
    new_momentum = 0.9 * momentum + tile_scale[:, None, None] * approximation
    new_vector_momentum = 0.9 * vector_momentum + vector_summed / replicas
    return (new_feedback, new_momentum, new_vector_momentum)


def solution(mesh):
    placed = (
        P("rep", "own", None, None),
        P("rep", "own", None, None),
        P("own", None, None),
        P("own"),
        P(),
        P(),
        P(),
        P(),
        P("rep", None, None),
        P(),
    )
    return jax.shard_map(
        local,
        mesh=mesh,
        in_specs=placed,
        out_specs=(P("rep", "own", None, None), P("own", None, None), P()),
        check_vma=False,
    )
```

```python
import jax
import jax.numpy as jnp
from jax import lax
from jax.sharding import PartitionSpec as P

TOP_PRECISION = lax.Precision.HIGHEST


def _bits(n):
    return (n - 1).bit_length()


def _pair_perm(n, j):
    return [(i, i ^ (1 << j)) for i in range(n)]


def swap_sum(x, axis):
    n = lax.axis_size(axis)
    for j in range(_bits(n)):
        x = x + lax.ppermute(x, axis, _pair_perm(n, j))
    return x


def _split_plan(shape, steps):
    dims = list(shape)
    plan = []
    for _ in range(steps):
        if dims[-1] > 128:
            axis = len(dims) - 1
        elif dims[-2] > 8:
            axis = len(dims) - 2
        elif dims[-1] % 2 == 0 and dims[-1] >= dims[-2]:
            axis = len(dims) - 1
        else:
            axis = len(dims) - 2
        assert dims[axis] % 2 == 0
        dims[axis] //= 2
        plan.append(axis)
    return plan


def _scatter_rows(parts, rows, count):
    slots = jnp.arange(count, dtype=rows.dtype)[:, None, None]
    table = None
    for i in range(parts.shape[0]):
        term = jnp.where(slots == rows[i], parts[i][None], 0.0)
        table = term if table is None else table + term
    return table


def table_rows(x, rows, n_rep, n_own):
    axes = ("rep", "own")
    count = n_rep * n_own
    index = lax.axis_index("rep") * n_own + lax.axis_index("own")
    core = index & 1
    own_bits = _bits(n_own)
    rest = list(range(1, own_bits)) + [own_bits + j for j in range(_bits(n_rep))]
    alt = list(rest)
    for i in range(0, len(alt) - 1, 2):
        alt[i], alt[i + 1] = alt[i + 1], alt[i]
    stages = [(0, 0)] + list(zip(rest, alt))
    tail = min(2, len(rest))
    halving = stages[: len(stages) - tail]
    pairing = stages[len(stages) - tail :]

    def perm_of(p0, p1):
        return [(i, i ^ (1 << (p0 if i % 2 == 0 else p1))) for i in range(count)]

    def bit_of(p0, p1):
        return (index >> jnp.where(core == 0, p0, p1)) & 1

    plan = _split_plan(x.shape, len(halving))
    bits = []
    cur = x
    for (p0, p1), axis in zip(halving, plan):
        bit = bit_of(p0, p1)
        half = cur.shape[axis] // 2
        keep = lax.dynamic_slice_in_dim(cur, bit * half, half, axis)
        send = lax.dynamic_slice_in_dim(cur, (1 - bit) * half, half, axis)
        cur = keep + lax.ppermute(send, axes, perm_of(p0, p1))
        bits.append(bit)
    for p0, p1 in pairing:
        cur = cur + lax.ppermute(cur, axes, perm_of(p0, p1))
    for (p0, p1), axis, bit in reversed(list(zip(halving, plan, bits))):
        other = lax.ppermute(cur, axes, perm_of(p0, p1))
        low = jnp.where(bit == 0, cur, other)
        high = jnp.where(bit == 0, other, cur)
        cur = jnp.concatenate([low, high], axis=axis)
    return cur.at[rows].get(mode="promise_in_bounds")


def local(
    gradient,
    feedback,
    momentum,
    tile_matrix,
    matrix_group,
    group_scale,
    start_basis,
    inverse_gram_factors,
    vector_grad,
    vector_momentum,
):
    replicas = lax.axis_size("rep")
    n_own = lax.axis_size("own")
    matrix_count = start_basis.shape[0]
    selector = (tile_matrix[:, None] == jnp.arange(matrix_count, dtype=jnp.int32)[None, :]).astype(
        jnp.float32
    )
    combined = gradient[0].astype(jnp.float32) + feedback[0]
    q_tiles = start_basis.at[tile_matrix].get(mode="promise_in_bounds")
    first_local = jnp.einsum("tkd,tds->tks", combined, q_tiles, precision=TOP_PRECISION)
    left_size = first_local.size
    carried = jnp.concatenate([first_local.reshape(-1), vector_grad[0].reshape(-1)])
    carried = swap_sum(carried, "rep")
    first_left = carried[:left_size].reshape(first_local.shape) / replicas
    vector_summed = carried[left_size:].reshape(vector_grad.shape[1:])
    mix_first = inverse_gram_factors[0].at[tile_matrix].get(mode="promise_in_bounds")
    first_ortho = jnp.einsum("tks,tsa->tka", first_left, mix_first, precision=TOP_PRECISION)
    first_parts = jnp.einsum("tkd,tks->tsd", combined, first_ortho, precision=TOP_PRECISION)
    first_table = _scatter_rows(first_parts, tile_matrix, matrix_count)
    first_rows = table_rows(first_table, tile_matrix, replicas, n_own) / replicas
    mix_right = inverse_gram_factors[1].at[tile_matrix].get(mode="promise_in_bounds")
    right_rows = jnp.einsum("tjw,tjd->twd", mix_right, first_rows, precision=TOP_PRECISION)
    second_local = jnp.einsum("tkd,tsd->tks", combined, right_rows, precision=TOP_PRECISION)
    second_left = swap_sum(second_local, "rep") / replicas
    mix_second = inverse_gram_factors[2].at[tile_matrix].get(mode="promise_in_bounds")
    second_ortho = jnp.einsum("tks,tsa->tka", second_left, mix_second, precision=TOP_PRECISION)
    second_parts = jnp.einsum("tkd,tks->tsd", combined, second_ortho, precision=TOP_PRECISION)
    second_table = _scatter_rows(second_parts, tile_matrix, matrix_count)
    back_rows = table_rows(second_table, tile_matrix, replicas, n_own) / replicas
    approximation = jnp.einsum("tks,tsd->tkd", second_ortho, back_rows, precision=TOP_PRECISION)
    new_feedback = (combined - approximation)[None]
    group_select = (
        matrix_group[:, None] == jnp.arange(group_scale.shape[0], dtype=jnp.int32)[None, :]
    ).astype(jnp.float32)
    matrix_scale = jnp.dot(group_select, group_scale, precision=TOP_PRECISION)
    tile_scale = jnp.dot(selector, matrix_scale, precision=TOP_PRECISION)
    new_momentum = 0.9 * momentum + tile_scale[:, None, None] * approximation
    new_vector_momentum = 0.9 * vector_momentum + vector_summed / replicas
    return (new_feedback, new_momentum, new_vector_momentum)


def solution(mesh):
    placed = (
        P("rep", "own", None, None),
        P("rep", "own", None, None),
        P("own", None, None),
        P("own"),
        P(),
        P(),
        P(),
        P(),
        P("rep", None, None),
        P(),
    )
    return jax.shard_map(
        local,
        mesh=mesh,
        in_specs=placed,
        out_specs=(P("rep", "own", None, None), P("own", None, None), P()),
        check_vma=False,
    )
```

```python
import jax
import jax.numpy as jnp
from jax import lax
from jax.sharding import PartitionSpec as P

TOP_PRECISION = lax.Precision.HIGHEST


def _bits(n):
    return (n - 1).bit_length()


def _pair_perm(n, j):
    return [(i, i ^ (1 << j)) for i in range(n)]


def swap_sum(x, axis):
    n = lax.axis_size(axis)
    for j in range(_bits(n)):
        x = x + lax.ppermute(x, axis, _pair_perm(n, j))
    return x


def _split_plan(shape, steps):
    dims = list(shape)
    plan = []
    for _ in range(steps):
        if dims[-1] > 128:
            axis = len(dims) - 1
        elif dims[-2] > 8:
            axis = len(dims) - 2
        elif dims[-1] % 2 == 0 and dims[-1] >= dims[-2]:
            axis = len(dims) - 1
        else:
            axis = len(dims) - 2
        assert dims[axis] % 2 == 0
        dims[axis] //= 2
        plan.append(axis)
    return plan


def _scalar_rows(rows, count):
    width = max(1, (count - 1).bit_length())
    n = rows.shape[0]
    if n * width > 31:
        return [rows[i] for i in range(n)]
    fields = jnp.left_shift(rows, jnp.arange(n, dtype=rows.dtype) * width)
    packed = jnp.sum(fields)
    return [(packed >> (i * width)) & ((1 << width) - 1) for i in range(n)]


def _pick_rows(table, rows):
    return jnp.stack([lax.dynamic_index_in_dim(table, r, 0, keepdims=False) for r in rows])


def _scatter_rows(parts, rows, count):
    table = jnp.zeros((count,) + parts.shape[1:], parts.dtype)
    for i, r in enumerate(rows):
        slab = lax.dynamic_index_in_dim(table, r, 0, keepdims=True)
        table = lax.dynamic_update_index_in_dim(table, slab + parts[i : i + 1], r, 0)
    return table


def table_rows(x, rows, n_rep, n_own):
    axes = ("rep", "own")
    count = n_rep * n_own
    index = lax.axis_index("rep") * n_own + lax.axis_index("own")
    core = index & 1
    own_bits = _bits(n_own)
    rest = list(range(1, own_bits)) + [own_bits + j for j in range(_bits(n_rep))]
    alt = list(rest)
    for i in range(0, len(alt) - 1, 2):
        alt[i], alt[i + 1] = alt[i + 1], alt[i]
    stages = [(0, 0)] + list(zip(rest, alt))
    tail = min(2, len(rest))
    halving = stages[: len(stages) - tail]
    pairing = stages[len(stages) - tail :]

    def perm_of(p0, p1):
        return [(i, i ^ (1 << (p0 if i % 2 == 0 else p1))) for i in range(count)]

    def bit_of(p0, p1):
        return (index >> jnp.where(core == 0, p0, p1)) & 1

    plan = _split_plan(x.shape, len(halving))
    bits = []
    cur = x
    for (p0, p1), axis in zip(halving, plan):
        bit = bit_of(p0, p1)
        half = cur.shape[axis] // 2
        keep = lax.dynamic_slice_in_dim(cur, bit * half, half, axis)
        send = lax.dynamic_slice_in_dim(cur, (1 - bit) * half, half, axis)
        cur = keep + lax.ppermute(send, axes, perm_of(p0, p1))
        bits.append(bit)
    for p0, p1 in pairing:
        cur = cur + lax.ppermute(cur, axes, perm_of(p0, p1))
    steps_back = list(reversed(list(zip(halving, plan, bits))))
    for index_step, ((p0, p1), axis, bit) in enumerate(steps_back):
        other = lax.ppermute(cur, axes, perm_of(p0, p1))
        if index_step == len(steps_back) - 1:
            cur = _pick_rows(cur, rows)
            other = _pick_rows(other, rows)
        low = jnp.where(bit == 0, cur, other)
        high = jnp.where(bit == 0, other, cur)
        cur = jnp.concatenate([low, high], axis=axis)
    if not steps_back:
        cur = _pick_rows(cur, rows)
    return cur


def local(
    gradient,
    feedback,
    momentum,
    tile_matrix,
    matrix_group,
    group_scale,
    start_basis,
    inverse_gram_factors,
    vector_grad,
    vector_momentum,
):
    replicas = lax.axis_size("rep")
    n_own = lax.axis_size("own")
    matrix_count = start_basis.shape[0]
    selector = (tile_matrix[:, None] == jnp.arange(matrix_count, dtype=jnp.int32)[None, :]).astype(
        jnp.float32
    )
    combined = gradient[0].astype(jnp.float32) + feedback[0]
    tile_rows = _scalar_rows(tile_matrix, matrix_count)
    q_tiles = _pick_rows(start_basis, tile_rows)
    first_local = jnp.einsum("tkd,tds->tks", combined, q_tiles, precision=TOP_PRECISION)
    left_size = first_local.size
    carried = jnp.concatenate([first_local.reshape(-1), vector_grad[0].reshape(-1)])
    carried = swap_sum(carried, "rep")
    first_left = carried[:left_size].reshape(first_local.shape) / replicas
    vector_summed = carried[left_size:].reshape(vector_grad.shape[1:])
    mix_first = _pick_rows(inverse_gram_factors[0], tile_rows)
    first_ortho = jnp.einsum("tks,tsa->tka", first_left, mix_first, precision=TOP_PRECISION)
    first_parts = jnp.einsum("tkd,tks->tsd", combined, first_ortho, precision=TOP_PRECISION)
    first_table = _scatter_rows(first_parts, tile_rows, matrix_count)
    first_rows = table_rows(first_table, tile_rows, replicas, n_own) / replicas
    mix_right = _pick_rows(inverse_gram_factors[1], tile_rows)
    right_rows = jnp.einsum("tjw,tjd->twd", mix_right, first_rows, precision=TOP_PRECISION)
    second_local = jnp.einsum("tkd,tsd->tks", combined, right_rows, precision=TOP_PRECISION)
    second_left = swap_sum(second_local, "rep") / replicas
    mix_second = _pick_rows(inverse_gram_factors[2], tile_rows)
    second_ortho = jnp.einsum("tks,tsa->tka", second_left, mix_second, precision=TOP_PRECISION)
    second_parts = jnp.einsum("tkd,tks->tsd", combined, second_ortho, precision=TOP_PRECISION)
    second_table = _scatter_rows(second_parts, tile_rows, matrix_count)
    back_rows = table_rows(second_table, tile_rows, replicas, n_own) / replicas
    approximation = jnp.einsum("tks,tsd->tkd", second_ortho, back_rows, precision=TOP_PRECISION)
    new_feedback = (combined - approximation)[None]
    group_select = (
        matrix_group[:, None] == jnp.arange(group_scale.shape[0], dtype=jnp.int32)[None, :]
    ).astype(jnp.float32)
    matrix_scale = jnp.dot(group_select, group_scale, precision=TOP_PRECISION)
    tile_scale = jnp.dot(selector, matrix_scale, precision=TOP_PRECISION)
    new_momentum = 0.9 * momentum + tile_scale[:, None, None] * approximation
    new_vector_momentum = 0.9 * vector_momentum + vector_summed / replicas
    return (new_feedback, new_momentum, new_vector_momentum)


def solution(mesh):
    placed = (
        P("rep", "own", None, None),
        P("rep", "own", None, None),
        P("own", None, None),
        P("own"),
        P(),
        P(),
        P(),
        P(),
        P("rep", None, None),
        P(),
    )
    return jax.shard_map(
        local,
        mesh=mesh,
        in_specs=placed,
        out_specs=(P("rep", "own", None, None), P("own", None, None), P()),
        check_vma=False,
    )
```

```python
import jax
import jax.numpy as jnp
from jax import lax
from jax.sharding import PartitionSpec as P

TOP_PRECISION = lax.Precision.HIGHEST


def _bits(n):
    return (n - 1).bit_length()


def _pair_perm(n, j):
    return [(i, i ^ (1 << j)) for i in range(n)]


def swap_sum(x, axis):
    n = lax.axis_size(axis)
    for j in range(_bits(n)):
        x = x + lax.ppermute(x, axis, _pair_perm(n, j))
    return x


def _split_plan(shape, steps):
    dims = list(shape)
    plan = []
    for _ in range(steps):
        if dims[-1] > 128:
            axis = len(dims) - 1
        elif dims[-2] > 8:
            axis = len(dims) - 2
        elif dims[-1] % 2 == 0 and dims[-1] >= dims[-2]:
            axis = len(dims) - 1
        else:
            axis = len(dims) - 2
        assert dims[axis] % 2 == 0
        dims[axis] //= 2
        plan.append(axis)
    return plan


def _scalar_rows(rows, count):
    width = max(1, (count - 1).bit_length())
    n = rows.shape[0]
    if n * width > 31:
        return [rows[i] for i in range(n)]
    fields = jnp.left_shift(rows, jnp.arange(n, dtype=rows.dtype) * width)
    packed = jnp.sum(fields)
    return [(packed >> (i * width)) & ((1 << width) - 1) for i in range(n)]


def _pick_rows(table, rows):
    return jnp.stack([lax.dynamic_index_in_dim(table, r, 0, keepdims=False) for r in rows])


def _scatter_rows(parts, rows, count):
    table = jnp.zeros((count,) + parts.shape[1:], parts.dtype)
    for i, r in enumerate(rows):
        slab = lax.dynamic_index_in_dim(table, r, 0, keepdims=True)
        table = lax.dynamic_update_index_in_dim(table, slab + parts[i : i + 1], r, 0)
    return table


def table_rows(x, rows, n_rep, n_own):
    axes = ("rep", "own")
    count = n_rep * n_own
    index = lax.axis_index("rep") * n_own + lax.axis_index("own")
    core = index & 1
    own_bits = _bits(n_own)
    rest = list(range(1, own_bits)) + [own_bits + j for j in range(_bits(n_rep))]
    alt = list(rest)
    for i in range(0, len(alt) - 1, 2):
        alt[i], alt[i + 1] = alt[i + 1], alt[i]
    stages = [(0, 0)] + list(zip(rest, alt))
    tail = min(3, len(rest))
    halving = stages[: len(stages) - tail]
    pairing = stages[len(stages) - tail :]

    def perm_of(p0, p1):
        return [(i, i ^ (1 << (p0 if i % 2 == 0 else p1))) for i in range(count)]

    def bit_of(p0, p1):
        return (index >> jnp.where(core == 0, p0, p1)) & 1

    plan = _split_plan(x.shape, len(halving))
    bits = []
    cur = x
    for (p0, p1), axis in zip(halving, plan):
        bit = bit_of(p0, p1)
        half = cur.shape[axis] // 2
        keep = lax.dynamic_slice_in_dim(cur, bit * half, half, axis)
        send = lax.dynamic_slice_in_dim(cur, (1 - bit) * half, half, axis)
        cur = keep + lax.ppermute(send, axes, perm_of(p0, p1))
        bits.append(bit)
    for p0, p1 in pairing:
        cur = cur + lax.ppermute(cur, axes, perm_of(p0, p1))
    steps_back = list(reversed(list(zip(halving, plan, bits))))
    for index_step, ((p0, p1), axis, bit) in enumerate(steps_back):
        other = lax.ppermute(cur, axes, perm_of(p0, p1))
        if index_step == len(steps_back) - 1:
            cur = _pick_rows(cur, rows)
            other = _pick_rows(other, rows)
        low = jnp.where(bit == 0, cur, other)
        high = jnp.where(bit == 0, other, cur)
        cur = jnp.concatenate([low, high], axis=axis)
    if not steps_back:
        cur = _pick_rows(cur, rows)
    return cur


def local(
    gradient,
    feedback,
    momentum,
    tile_matrix,
    matrix_group,
    group_scale,
    start_basis,
    inverse_gram_factors,
    vector_grad,
    vector_momentum,
):
    replicas = lax.axis_size("rep")
    n_own = lax.axis_size("own")
    matrix_count = start_basis.shape[0]
    selector = (tile_matrix[:, None] == jnp.arange(matrix_count, dtype=jnp.int32)[None, :]).astype(
        jnp.float32
    )
    combined = gradient[0].astype(jnp.float32) + feedback[0]
    tile_rows = _scalar_rows(tile_matrix, matrix_count)
    q_tiles = _pick_rows(start_basis, tile_rows)
    first_local = jnp.einsum("tkd,tds->tks", combined, q_tiles, precision=TOP_PRECISION)
    left_size = first_local.size
    carried = jnp.concatenate([first_local.reshape(-1), vector_grad[0].reshape(-1)])
    carried = swap_sum(carried, "rep")
    first_left = carried[:left_size].reshape(first_local.shape) / replicas
    vector_summed = carried[left_size:].reshape(vector_grad.shape[1:])
    mix_first = _pick_rows(inverse_gram_factors[0], tile_rows)
    first_ortho = jnp.einsum("tks,tsa->tka", first_left, mix_first, precision=TOP_PRECISION)
    first_parts = jnp.einsum("tkd,tks->tsd", combined, first_ortho, precision=TOP_PRECISION)
    first_table = _scatter_rows(first_parts, tile_rows, matrix_count)
    first_rows = table_rows(first_table, tile_rows, replicas, n_own) / replicas
    mix_right = _pick_rows(inverse_gram_factors[1], tile_rows)
    right_rows = jnp.einsum("tjw,tjd->twd", mix_right, first_rows, precision=TOP_PRECISION)
    second_local = jnp.einsum("tkd,tsd->tks", combined, right_rows, precision=TOP_PRECISION)
    second_left = swap_sum(second_local, "rep") / replicas
    mix_second = _pick_rows(inverse_gram_factors[2], tile_rows)
    second_ortho = jnp.einsum("tks,tsa->tka", second_left, mix_second, precision=TOP_PRECISION)
    second_parts = jnp.einsum("tkd,tks->tsd", combined, second_ortho, precision=TOP_PRECISION)
    second_table = _scatter_rows(second_parts, tile_rows, matrix_count)
    back_rows = table_rows(second_table, tile_rows, replicas, n_own) / replicas
    approximation = jnp.einsum("tks,tsd->tkd", second_ortho, back_rows, precision=TOP_PRECISION)
    new_feedback = (combined - approximation)[None]
    group_select = (
        matrix_group[:, None] == jnp.arange(group_scale.shape[0], dtype=jnp.int32)[None, :]
    ).astype(jnp.float32)
    matrix_scale = jnp.dot(group_select, group_scale, precision=TOP_PRECISION)
    tile_scale = jnp.dot(selector, matrix_scale, precision=TOP_PRECISION)
    new_momentum = 0.9 * momentum + tile_scale[:, None, None] * approximation
    new_vector_momentum = 0.9 * vector_momentum + vector_summed / replicas
    return (new_feedback, new_momentum, new_vector_momentum)


def solution(mesh):
    placed = (
        P("rep", "own", None, None),
        P("rep", "own", None, None),
        P("own", None, None),
        P("own"),
        P(),
        P(),
        P(),
        P(),
        P("rep", None, None),
        P(),
    )
    return jax.shard_map(
        local,
        mesh=mesh,
        in_specs=placed,
        out_specs=(P("rep", "own", None, None), P("own", None, None), P()),
        check_vma=False,
    )
```

```python
import jax
import jax.numpy as jnp
from jax import lax
from jax.sharding import PartitionSpec as P

TOP_PRECISION = lax.Precision.HIGHEST
WIDE_PRECISION = lax.Precision.HIGH


def _bits(n):
    return (n - 1).bit_length()


def _pair_perm(n, j):
    return [(i, i ^ (1 << j)) for i in range(n)]


def swap_sum(x, axis):
    n = lax.axis_size(axis)
    for j in range(_bits(n)):
        x = x + lax.ppermute(x, axis, _pair_perm(n, j))
    return x


def _split_plan(shape, steps):
    dims = list(shape)
    plan = []
    for _ in range(steps):
        if dims[-1] > 128:
            axis = len(dims) - 1
        elif dims[-2] > 8:
            axis = len(dims) - 2
        elif dims[-1] % 2 == 0 and dims[-1] >= dims[-2]:
            axis = len(dims) - 1
        else:
            axis = len(dims) - 2
        assert dims[axis] % 2 == 0
        dims[axis] //= 2
        plan.append(axis)
    return plan


def _scalar_rows(rows, count):
    width = max(1, (count - 1).bit_length())
    n = rows.shape[0]
    if n * width > 31:
        return [rows[i] for i in range(n)]
    fields = jnp.left_shift(rows, jnp.arange(n, dtype=rows.dtype) * width)
    packed = jnp.sum(fields)
    return [(packed >> (i * width)) & ((1 << width) - 1) for i in range(n)]


def _pick_rows(table, rows):
    return jnp.stack([lax.dynamic_index_in_dim(table, r, 0, keepdims=False) for r in rows])


def _scatter_rows(parts, rows, count):
    table = jnp.zeros((count,) + parts.shape[1:], parts.dtype)
    for i, r in enumerate(rows):
        slab = lax.dynamic_index_in_dim(table, r, 0, keepdims=True)
        table = lax.dynamic_update_index_in_dim(table, slab + parts[i : i + 1], r, 0)
    return table


def table_rows(x, rows, n_rep, n_own):
    axes = ("rep", "own")
    count = n_rep * n_own
    index = lax.axis_index("rep") * n_own + lax.axis_index("own")
    core = index & 1
    own_bits = _bits(n_own)
    rest = list(range(1, own_bits)) + [own_bits + j for j in range(_bits(n_rep))]
    alt = list(rest)
    for i in range(0, len(alt) - 1, 2):
        alt[i], alt[i + 1] = alt[i + 1], alt[i]
    stages = [(0, 0)] + list(zip(rest, alt))
    tail = min(2, len(rest))
    halving = stages[: len(stages) - tail]
    pairing = stages[len(stages) - tail :]

    def perm_of(p0, p1):
        return [(i, i ^ (1 << (p0 if i % 2 == 0 else p1))) for i in range(count)]

    def bit_of(p0, p1):
        return (index >> jnp.where(core == 0, p0, p1)) & 1

    plan = _split_plan(x.shape, len(halving))
    bits = []
    cur = x
    for (p0, p1), axis in zip(halving, plan):
        bit = bit_of(p0, p1)
        half = cur.shape[axis] // 2
        keep = lax.dynamic_slice_in_dim(cur, bit * half, half, axis)
        send = lax.dynamic_slice_in_dim(cur, (1 - bit) * half, half, axis)
        cur = keep + lax.ppermute(send, axes, perm_of(p0, p1))
        bits.append(bit)
    for p0, p1 in pairing:
        cur = cur + lax.ppermute(cur, axes, perm_of(p0, p1))
    steps_back = list(reversed(list(zip(halving, plan, bits))))
    for index_step, ((p0, p1), axis, bit) in enumerate(steps_back):
        other = lax.ppermute(cur, axes, perm_of(p0, p1))
        if index_step == len(steps_back) - 1:
            cur = _pick_rows(cur, rows)
            other = _pick_rows(other, rows)
        low = jnp.where(bit == 0, cur, other)
        high = jnp.where(bit == 0, other, cur)
        cur = jnp.concatenate([low, high], axis=axis)
    if not steps_back:
        cur = _pick_rows(cur, rows)
    return cur


def local(
    gradient,
    feedback,
    momentum,
    tile_matrix,
    matrix_group,
    group_scale,
    start_basis,
    inverse_gram_factors,
    vector_grad,
    vector_momentum,
):
    replicas = lax.axis_size("rep")
    n_own = lax.axis_size("own")
    matrix_count = start_basis.shape[0]
    selector = (tile_matrix[:, None] == jnp.arange(matrix_count, dtype=jnp.int32)[None, :]).astype(
        jnp.float32
    )
    combined = gradient[0].astype(jnp.float32) + feedback[0]
    tile_rows = _scalar_rows(tile_matrix, matrix_count)
    q_tiles = _pick_rows(start_basis, tile_rows)
    first_local = jnp.einsum("tkd,tds->tks", combined, q_tiles, precision=WIDE_PRECISION)
    left_size = first_local.size
    carried = jnp.concatenate([first_local.reshape(-1), vector_grad[0].reshape(-1)])
    carried = swap_sum(carried, "rep")
    first_left = carried[:left_size].reshape(first_local.shape) / replicas
    vector_summed = carried[left_size:].reshape(vector_grad.shape[1:])
    mix_first = _pick_rows(inverse_gram_factors[0], tile_rows)
    first_ortho = jnp.einsum("tks,tsa->tka", first_left, mix_first, precision=TOP_PRECISION)
    first_parts = jnp.einsum("tkd,tks->tsd", combined, first_ortho, precision=WIDE_PRECISION)
    first_table = _scatter_rows(first_parts, tile_rows, matrix_count)
    first_rows = table_rows(first_table, tile_rows, replicas, n_own) / replicas
    mix_right = _pick_rows(inverse_gram_factors[1], tile_rows)
    right_rows = jnp.einsum("tjw,tjd->twd", mix_right, first_rows, precision=TOP_PRECISION)
    second_local = jnp.einsum("tkd,tsd->tks", combined, right_rows, precision=WIDE_PRECISION)
    second_left = swap_sum(second_local, "rep") / replicas
    mix_second = _pick_rows(inverse_gram_factors[2], tile_rows)
    second_ortho = jnp.einsum("tks,tsa->tka", second_left, mix_second, precision=TOP_PRECISION)
    second_parts = jnp.einsum("tkd,tks->tsd", combined, second_ortho, precision=WIDE_PRECISION)
    second_table = _scatter_rows(second_parts, tile_rows, matrix_count)
    back_rows = table_rows(second_table, tile_rows, replicas, n_own) / replicas
    approximation = jnp.einsum("tks,tsd->tkd", second_ortho, back_rows, precision=WIDE_PRECISION)
    new_feedback = (combined - approximation)[None]
    group_select = (
        matrix_group[:, None] == jnp.arange(group_scale.shape[0], dtype=jnp.int32)[None, :]
    ).astype(jnp.float32)
    matrix_scale = jnp.dot(group_select, group_scale, precision=TOP_PRECISION)
    tile_scale = jnp.dot(selector, matrix_scale, precision=TOP_PRECISION)
    new_momentum = 0.9 * momentum + tile_scale[:, None, None] * approximation
    new_vector_momentum = 0.9 * vector_momentum + vector_summed / replicas
    return (new_feedback, new_momentum, new_vector_momentum)


def solution(mesh):
    placed = (
        P("rep", "own", None, None),
        P("rep", "own", None, None),
        P("own", None, None),
        P("own"),
        P(),
        P(),
        P(),
        P(),
        P("rep", None, None),
        P(),
    )
    return jax.shard_map(
        local,
        mesh=mesh,
        in_specs=placed,
        out_specs=(P("rep", "own", None, None), P("own", None, None), P()),
        check_vma=False,
    )
```

```python
import jax
import jax.numpy as jnp
from jax import lax
from jax.sharding import PartitionSpec as P

TOP_PRECISION = lax.Precision.HIGHEST
WIDE_PRECISION = lax.Precision.HIGH


def _bits(n):
    return (n - 1).bit_length()


def _pair_perm(n, j):
    return [(i, i ^ (1 << j)) for i in range(n)]


def swap_sum(x, axis):
    n = lax.axis_size(axis)
    for j in range(_bits(n)):
        x = x + lax.ppermute(x, axis, _pair_perm(n, j))
    return x


def _split_plan(shape, steps):
    dims = list(shape)
    plan = []
    for _ in range(steps):
        if dims[-1] > 128:
            axis = len(dims) - 1
        elif dims[-2] > 8:
            axis = len(dims) - 2
        elif dims[-1] % 2 == 0 and dims[-1] >= dims[-2]:
            axis = len(dims) - 1
        else:
            axis = len(dims) - 2
        assert dims[axis] % 2 == 0
        dims[axis] //= 2
        plan.append(axis)
    return plan


def _scalar_rows(rows, count):
    width = max(1, (count - 1).bit_length())
    n = rows.shape[0]
    if n * width > 31:
        return [rows[i] for i in range(n)]
    fields = jnp.left_shift(rows, jnp.arange(n, dtype=rows.dtype) * width)
    packed = jnp.sum(fields)
    return [(packed >> (i * width)) & ((1 << width) - 1) for i in range(n)]


def _pick_rows(table, rows):
    return jnp.stack([lax.dynamic_index_in_dim(table, r, 0, keepdims=False) for r in rows])


def _scatter_rows(parts, rows, count):
    table = jnp.zeros((count,) + parts.shape[1:], parts.dtype)
    for i, r in enumerate(rows):
        slab = lax.dynamic_index_in_dim(table, r, 0, keepdims=True)
        table = lax.dynamic_update_index_in_dim(table, slab + parts[i : i + 1], r, 0)
    return table


def table_rows(x, rows, n_rep, n_own):
    axes = ("rep", "own")
    count = n_rep * n_own
    index = lax.axis_index("rep") * n_own + lax.axis_index("own")
    core = index & 1
    own_bits = _bits(n_own)
    rest = list(range(1, own_bits)) + [own_bits + j for j in range(_bits(n_rep))]
    alt = list(rest)
    for i in range(0, len(alt) - 1, 2):
        alt[i], alt[i + 1] = alt[i + 1], alt[i]
    stages = [(0, 0)] + list(zip(rest, alt))
    tail = min(2, len(rest))
    halving = stages[: len(stages) - tail]
    pairing = stages[len(stages) - tail :]

    def perm_of(p0, p1):
        return [(i, i ^ (1 << (p0 if i % 2 == 0 else p1))) for i in range(count)]

    def bit_of(p0, p1):
        return (index >> jnp.where(core == 0, p0, p1)) & 1

    plan = _split_plan(x.shape, len(halving))
    bits = []
    cur = x
    for (p0, p1), axis in zip(halving, plan):
        bit = bit_of(p0, p1)
        half = cur.shape[axis] // 2
        keep = lax.dynamic_slice_in_dim(cur, bit * half, half, axis)
        send = lax.dynamic_slice_in_dim(cur, (1 - bit) * half, half, axis)
        cur = keep + lax.ppermute(send, axes, perm_of(p0, p1))
        bits.append(bit)
    for p0, p1 in pairing:
        cur = cur + lax.ppermute(cur, axes, perm_of(p0, p1))
    steps_back = list(reversed(list(zip(halving, plan, bits))))
    for index_step, ((p0, p1), axis, bit) in enumerate(steps_back):
        other = lax.ppermute(cur, axes, perm_of(p0, p1))
        if index_step == len(steps_back) - 1:
            cur = _pick_rows(cur, rows)
            other = _pick_rows(other, rows)
        low = jnp.where(bit == 0, cur, other)
        high = jnp.where(bit == 0, other, cur)
        cur = jnp.concatenate([low, high], axis=axis)
    if not steps_back:
        cur = _pick_rows(cur, rows)
    return cur


def local(
    gradient,
    feedback,
    momentum,
    tile_matrix,
    matrix_group,
    group_scale,
    start_basis,
    inverse_gram_factors,
    vector_grad,
    vector_momentum,
):
    replicas = lax.axis_size("rep")
    n_own = lax.axis_size("own")
    matrix_count = start_basis.shape[0]
    selector = (tile_matrix[:, None] == jnp.arange(matrix_count, dtype=jnp.int32)[None, :]).astype(
        jnp.float32
    )
    combined = gradient[0].astype(jnp.float32) + feedback[0]
    tile_rows = _scalar_rows(tile_matrix, matrix_count)
    q_tiles = _pick_rows(start_basis, tile_rows)
    first_local = jnp.einsum("tkd,tds->tks", combined, q_tiles, precision=WIDE_PRECISION)
    left_size = first_local.size
    carried = jnp.concatenate([first_local.reshape(-1), vector_grad[0].reshape(-1)])
    carried = swap_sum(carried, "rep")
    first_left = carried[:left_size].reshape(first_local.shape) / replicas
    vector_summed = carried[left_size:].reshape(vector_grad.shape[1:])
    mix_first = _pick_rows(inverse_gram_factors[0], tile_rows)
    mix_right = _pick_rows(inverse_gram_factors[1], tile_rows)
    mix_second = _pick_rows(inverse_gram_factors[2], tile_rows)
    new_vector_momentum = 0.9 * vector_momentum + vector_summed / replicas
    group_select = (
        matrix_group[:, None] == jnp.arange(group_scale.shape[0], dtype=jnp.int32)[None, :]
    ).astype(jnp.float32)
    matrix_scale = jnp.dot(group_select, group_scale, precision=TOP_PRECISION)
    tile_scale = jnp.dot(selector, matrix_scale, precision=TOP_PRECISION)
    first_left, mix_right, mix_second, new_vector_momentum, tile_scale = lax.optimization_barrier(
        (first_left, mix_right, mix_second, new_vector_momentum, tile_scale)
    )
    first_ortho = jnp.einsum("tks,tsa->tka", first_left, mix_first, precision=TOP_PRECISION)
    first_parts = jnp.einsum("tkd,tks->tsd", combined, first_ortho, precision=WIDE_PRECISION)
    first_table = _scatter_rows(first_parts, tile_rows, matrix_count)
    first_rows = table_rows(first_table, tile_rows, replicas, n_own) / replicas
    right_rows = jnp.einsum("tjw,tjd->twd", mix_right, first_rows, precision=TOP_PRECISION)
    second_local = jnp.einsum("tkd,tsd->tks", combined, right_rows, precision=WIDE_PRECISION)
    second_left = swap_sum(second_local, "rep") / replicas
    second_ortho = jnp.einsum("tks,tsa->tka", second_left, mix_second, precision=TOP_PRECISION)
    second_parts = jnp.einsum("tkd,tks->tsd", combined, second_ortho, precision=WIDE_PRECISION)
    second_table = _scatter_rows(second_parts, tile_rows, matrix_count)
    back_rows = table_rows(second_table, tile_rows, replicas, n_own) / replicas
    approximation = jnp.einsum("tks,tsd->tkd", second_ortho, back_rows, precision=WIDE_PRECISION)
    new_feedback = (combined - approximation)[None]
    new_momentum = 0.9 * momentum + tile_scale[:, None, None] * approximation
    return (new_feedback, new_momentum, new_vector_momentum)


def solution(mesh):
    placed = (
        P("rep", "own", None, None),
        P("rep", "own", None, None),
        P("own", None, None),
        P("own"),
        P(),
        P(),
        P(),
        P(),
        P("rep", None, None),
        P(),
    )
    return jax.shard_map(
        local,
        mesh=mesh,
        in_specs=placed,
        out_specs=(P("rep", "own", None, None), P("own", None, None), P()),
        check_vma=False,
    )
```

```python
import jax
import jax.numpy as jnp
from jax import lax
from jax.sharding import PartitionSpec as P

TOP_PRECISION = lax.Precision.HIGHEST
WIDE_PRECISION = lax.Precision.HIGH


def _bits(n):
    return (n - 1).bit_length()


def _pair_perm(n, j):
    return [(i, i ^ (1 << j)) for i in range(n)]


def swap_sum(x, axis):
    n = lax.axis_size(axis)
    for j in range(_bits(n)):
        x = x + lax.ppermute(x, axis, _pair_perm(n, j))
    return x


def _split_plan(shape, steps):
    dims = list(shape)
    plan = []
    for _ in range(steps):
        if dims[-1] > 128:
            axis = len(dims) - 1
        elif dims[-2] > 8:
            axis = len(dims) - 2
        elif dims[-1] % 2 == 0 and dims[-1] >= dims[-2]:
            axis = len(dims) - 1
        else:
            axis = len(dims) - 2
        assert dims[axis] % 2 == 0
        dims[axis] //= 2
        plan.append(axis)
    return plan


def _scalar_rows(rows, count):
    width = max(1, (count - 1).bit_length())
    n = rows.shape[0]
    if n * width > 31:
        return [rows[i] for i in range(n)]
    fields = jnp.left_shift(rows, jnp.arange(n, dtype=rows.dtype) * width)
    packed = jnp.sum(fields)
    return [(packed >> (i * width)) & ((1 << width) - 1) for i in range(n)]


def _pick_rows(table, rows):
    return jnp.stack([lax.dynamic_index_in_dim(table, r, 0, keepdims=False) for r in rows])


def _scatter_rows(parts, rows, count):
    table = jnp.zeros((count,) + parts.shape[1:], parts.dtype)
    for i, r in enumerate(rows):
        slab = lax.dynamic_index_in_dim(table, r, 0, keepdims=True)
        table = lax.dynamic_update_index_in_dim(table, slab + parts[i : i + 1], r, 0)
    return table


def table_rows(x, rows, n_rep, n_own):
    axes = ("rep", "own")
    count = n_rep * n_own
    index = lax.axis_index("rep") * n_own + lax.axis_index("own")
    core = index & 1
    own_bits = _bits(n_own)
    rest = list(range(1, own_bits)) + [own_bits + j for j in range(_bits(n_rep))]
    alt = list(rest)
    for i in range(0, len(alt) - 1, 2):
        alt[i], alt[i + 1] = alt[i + 1], alt[i]
    stages = [(0, 0)] + list(zip(rest, alt))
    tail = min(2, len(rest))
    halving = stages[: len(stages) - tail]
    pairing = stages[len(stages) - tail :]

    def perm_of(p0, p1):
        return [(i, i ^ (1 << (p0 if i % 2 == 0 else p1))) for i in range(count)]

    def bit_of(p0, p1):
        return (index >> jnp.where(core == 0, p0, p1)) & 1

    plan = _split_plan(x.shape, len(halving))
    bits = []
    cur = x
    for (p0, p1), axis in zip(halving, plan):
        bit = bit_of(p0, p1)
        half = cur.shape[axis] // 2
        keep = lax.dynamic_slice_in_dim(cur, bit * half, half, axis)
        send = lax.dynamic_slice_in_dim(cur, (1 - bit) * half, half, axis)
        cur = keep + lax.ppermute(send, axes, perm_of(p0, p1))
        bits.append(bit)
    for p0, p1 in pairing:
        cur = cur + lax.ppermute(cur, axes, perm_of(p0, p1))
    steps_back = list(reversed(list(zip(halving, plan, bits))))
    for index_step, ((p0, p1), axis, bit) in enumerate(steps_back):
        other = lax.ppermute(cur, axes, perm_of(p0, p1))
        if index_step == len(steps_back) - 1:
            cur = _pick_rows(cur, rows)
            other = _pick_rows(other, rows)
        low = jnp.where(bit == 0, cur, other)
        high = jnp.where(bit == 0, other, cur)
        cur = jnp.concatenate([low, high], axis=axis)
    if not steps_back:
        cur = _pick_rows(cur, rows)
    return cur


def local(
    gradient,
    feedback,
    momentum,
    tile_matrix,
    matrix_group,
    group_scale,
    start_basis,
    inverse_gram_factors,
    vector_grad,
    vector_momentum,
):
    replicas = lax.axis_size("rep")
    n_own = lax.axis_size("own")
    matrix_count = start_basis.shape[0]
    selector = (tile_matrix[:, None] == jnp.arange(matrix_count, dtype=jnp.int32)[None, :]).astype(
        jnp.float32
    )
    combined = gradient[0].astype(jnp.float32) + feedback[0]
    tile_rows = _scalar_rows(tile_matrix, matrix_count)
    every_basis = jnp.einsum("tkd,mds->tkms", combined, start_basis, precision=WIDE_PRECISION)
    own_basis = tile_matrix[:, None, None] == jnp.arange(matrix_count, dtype=tile_matrix.dtype)[None, :, None]
    first_local = jnp.sum(jnp.where(own_basis[:, None, :, :], every_basis, 0.0), axis=2)
    left_size = first_local.size
    carried = jnp.concatenate([first_local.reshape(-1), vector_grad[0].reshape(-1)])
    carried = swap_sum(carried, "rep")
    first_left = carried[:left_size].reshape(first_local.shape) / replicas
    vector_summed = carried[left_size:].reshape(vector_grad.shape[1:])
    mix_first = _pick_rows(inverse_gram_factors[0], tile_rows)
    mix_right = _pick_rows(inverse_gram_factors[1], tile_rows)
    mix_second = _pick_rows(inverse_gram_factors[2], tile_rows)
    new_vector_momentum = 0.9 * vector_momentum + vector_summed / replicas
    group_select = (
        matrix_group[:, None] == jnp.arange(group_scale.shape[0], dtype=jnp.int32)[None, :]
    ).astype(jnp.float32)
    matrix_scale = jnp.dot(group_select, group_scale, precision=TOP_PRECISION)
    tile_scale = jnp.dot(selector, matrix_scale, precision=TOP_PRECISION)
    first_left, mix_right, mix_second, new_vector_momentum, tile_scale = lax.optimization_barrier(
        (first_left, mix_right, mix_second, new_vector_momentum, tile_scale)
    )
    first_ortho = jnp.einsum("tks,tsa->tka", first_left, mix_first, precision=TOP_PRECISION)
    first_parts = jnp.einsum("tkd,tks->tsd", combined, first_ortho, precision=WIDE_PRECISION)
    first_table = _scatter_rows(first_parts, tile_rows, matrix_count)
    first_rows = table_rows(first_table, tile_rows, replicas, n_own) / replicas
    right_rows = jnp.einsum("tjw,tjd->twd", mix_right, first_rows, precision=TOP_PRECISION)
    second_local = jnp.einsum("tkd,tsd->tks", combined, right_rows, precision=WIDE_PRECISION)
    second_left = swap_sum(second_local, "rep") / replicas
    second_ortho = jnp.einsum("tks,tsa->tka", second_left, mix_second, precision=TOP_PRECISION)
    second_parts = jnp.einsum("tkd,tks->tsd", combined, second_ortho, precision=WIDE_PRECISION)
    second_table = _scatter_rows(second_parts, tile_rows, matrix_count)
    back_rows = table_rows(second_table, tile_rows, replicas, n_own) / replicas
    approximation = jnp.einsum("tks,tsd->tkd", second_ortho, back_rows, precision=WIDE_PRECISION)
    new_feedback = (combined - approximation)[None]
    new_momentum = 0.9 * momentum + tile_scale[:, None, None] * approximation
    return (new_feedback, new_momentum, new_vector_momentum)


def solution(mesh):
    placed = (
        P("rep", "own", None, None),
        P("rep", "own", None, None),
        P("own", None, None),
        P("own"),
        P(),
        P(),
        P(),
        P(),
        P("rep", None, None),
        P(),
    )
    return jax.shard_map(
        local,
        mesh=mesh,
        in_specs=placed,
        out_specs=(P("rep", "own", None, None), P("own", None, None), P()),
        check_vma=False,
    )
```

```python
import jax
import jax.numpy as jnp
from jax import lax
from jax.sharding import PartitionSpec as P

TOP_PRECISION = lax.Precision.HIGHEST
WIDE_PRECISION = lax.Precision.HIGH


def _bits(n):
    return (n - 1).bit_length()


def _pair_perm(n, j):
    return [(i, i ^ (1 << j)) for i in range(n)]


def swap_sum(x, axis):
    n = lax.axis_size(axis)
    for j in range(_bits(n)):
        x = x + lax.ppermute(x, axis, _pair_perm(n, j))
    return x


def _split_plan(shape, steps):
    dims = list(shape)
    plan = []
    for _ in range(steps):
        if dims[-1] > 128:
            axis = len(dims) - 1
        elif dims[-2] > 8:
            axis = len(dims) - 2
        elif dims[-1] % 2 == 0 and dims[-1] >= dims[-2]:
            axis = len(dims) - 1
        else:
            axis = len(dims) - 2
        assert dims[axis] % 2 == 0
        dims[axis] //= 2
        plan.append(axis)
    return plan


def _scalar_rows(rows, count):
    width = max(1, (count - 1).bit_length())
    n = rows.shape[0]
    if n * width > 31:
        return [rows[i] for i in range(n)]
    fields = jnp.left_shift(rows, jnp.arange(n, dtype=rows.dtype) * width)
    packed = jnp.sum(fields)
    return [(packed >> (i * width)) & ((1 << width) - 1) for i in range(n)]


def _pick_rows(table, rows):
    return jnp.stack([lax.dynamic_index_in_dim(table, r, 0, keepdims=False) for r in rows])


def _scatter_rows(parts, rows, count):
    table = jnp.zeros((count,) + parts.shape[1:], parts.dtype)
    for i, r in enumerate(rows):
        slab = lax.dynamic_index_in_dim(table, r, 0, keepdims=True)
        table = lax.dynamic_update_index_in_dim(table, slab + parts[i : i + 1], r, 0)
    return table


def table_rows(x, rows, n_rep, n_own):
    axes = ("rep", "own")
    count = n_rep * n_own
    index = lax.axis_index("rep") * n_own + lax.axis_index("own")
    core = index & 1
    own_bits = _bits(n_own)
    rest = list(range(1, own_bits)) + [own_bits + j for j in range(_bits(n_rep))]
    alt = list(rest)
    for i in range(0, len(alt) - 1, 2):
        alt[i], alt[i + 1] = alt[i + 1], alt[i]
    stages = [(0, 0)] + list(zip(rest, alt))
    tail = min(2, len(rest))
    halving = stages[: len(stages) - tail]
    pairing = stages[len(stages) - tail :]

    def perm_of(p0, p1):
        return [(i, i ^ (1 << (p0 if i % 2 == 0 else p1))) for i in range(count)]

    def bit_of(p0, p1):
        return (index >> jnp.where(core == 0, p0, p1)) & 1

    plan = _split_plan(x.shape, len(halving))
    bits = []
    cur = x
    for (p0, p1), axis in zip(halving, plan):
        bit = bit_of(p0, p1)
        half = cur.shape[axis] // 2
        keep = lax.dynamic_slice_in_dim(cur, bit * half, half, axis)
        send = lax.dynamic_slice_in_dim(cur, (1 - bit) * half, half, axis)
        cur = keep + lax.ppermute(send, axes, perm_of(p0, p1))
        bits.append(bit)
    if len(pairing) == 2:
        (a0, a1), (b0, b1) = pairing

        def group_perm(k):
            pairs = []
            for i in range(count):
                pa, pb = (a0, b0) if i % 2 == 0 else (a1, b1)
                pairs.append((i, i ^ (((k & 1) << pa) | ((k >> 1) << pb))))
            return pairs

        place = bit_of(a0, a1) + 2 * bit_of(b0, b1)
        held = [cur] + [lax.ppermute(cur, axes, group_perm(k)) for k in (1, 2, 3)]
        total = None
        for member in range(4):
            term = lax.select_n(place ^ member, *held)
            total = term if total is None else total + term
        cur = total
    else:
        for p0, p1 in pairing:
            cur = cur + lax.ppermute(cur, axes, perm_of(p0, p1))
    steps_back = list(reversed(list(zip(halving, plan, bits))))
    for index_step, ((p0, p1), axis, bit) in enumerate(steps_back):
        other = lax.ppermute(cur, axes, perm_of(p0, p1))
        if index_step == len(steps_back) - 1:
            cur = _pick_rows(cur, rows)
            other = _pick_rows(other, rows)
        low = jnp.where(bit == 0, cur, other)
        high = jnp.where(bit == 0, other, cur)
        cur = jnp.concatenate([low, high], axis=axis)
    if not steps_back:
        cur = _pick_rows(cur, rows)
    return cur


def local(
    gradient,
    feedback,
    momentum,
    tile_matrix,
    matrix_group,
    group_scale,
    start_basis,
    inverse_gram_factors,
    vector_grad,
    vector_momentum,
):
    replicas = lax.axis_size("rep")
    n_own = lax.axis_size("own")
    matrix_count = start_basis.shape[0]
    selector = (tile_matrix[:, None] == jnp.arange(matrix_count, dtype=jnp.int32)[None, :]).astype(
        jnp.float32
    )
    combined = gradient[0].astype(jnp.float32) + feedback[0]
    tile_rows = _scalar_rows(tile_matrix, matrix_count)
    q_tiles = _pick_rows(start_basis, tile_rows)
    first_local = jnp.einsum("tkd,tds->tks", combined, q_tiles, precision=WIDE_PRECISION)
    left_size = first_local.size
    carried = jnp.concatenate([first_local.reshape(-1), vector_grad[0].reshape(-1)])
    carried = swap_sum(carried, "rep")
    first_left = carried[:left_size].reshape(first_local.shape) / replicas
    vector_summed = carried[left_size:].reshape(vector_grad.shape[1:])
    mix_first = _pick_rows(inverse_gram_factors[0], tile_rows)
    mix_right = _pick_rows(inverse_gram_factors[1], tile_rows)
    mix_second = _pick_rows(inverse_gram_factors[2], tile_rows)
    new_vector_momentum = 0.9 * vector_momentum + vector_summed / replicas
    group_select = (
        matrix_group[:, None] == jnp.arange(group_scale.shape[0], dtype=jnp.int32)[None, :]
    ).astype(jnp.float32)
    matrix_scale = jnp.dot(group_select, group_scale, precision=TOP_PRECISION)
    tile_scale = jnp.dot(selector, matrix_scale, precision=TOP_PRECISION)
    first_left, mix_right, mix_second, new_vector_momentum, tile_scale = lax.optimization_barrier(
        (first_left, mix_right, mix_second, new_vector_momentum, tile_scale)
    )
    first_ortho = jnp.einsum("tks,tsa->tka", first_left, mix_first, precision=TOP_PRECISION)
    first_parts = jnp.einsum("tkd,tks->tsd", combined, first_ortho, precision=WIDE_PRECISION)
    first_table = _scatter_rows(first_parts, tile_rows, matrix_count)
    first_rows = table_rows(first_table, tile_rows, replicas, n_own) / replicas
    right_rows = jnp.einsum("tjw,tjd->twd", mix_right, first_rows, precision=TOP_PRECISION)
    second_local = jnp.einsum("tkd,tsd->tks", combined, right_rows, precision=WIDE_PRECISION)
    second_left = swap_sum(second_local, "rep") / replicas
    second_ortho = jnp.einsum("tks,tsa->tka", second_left, mix_second, precision=TOP_PRECISION)
    second_parts = jnp.einsum("tkd,tks->tsd", combined, second_ortho, precision=WIDE_PRECISION)
    second_table = _scatter_rows(second_parts, tile_rows, matrix_count)
    back_rows = table_rows(second_table, tile_rows, replicas, n_own) / replicas
    approximation = jnp.einsum("tks,tsd->tkd", second_ortho, back_rows, precision=WIDE_PRECISION)
    new_feedback = (combined - approximation)[None]
    new_momentum = 0.9 * momentum + tile_scale[:, None, None] * approximation
    return (new_feedback, new_momentum, new_vector_momentum)


def solution(mesh):
    placed = (
        P("rep", "own", None, None),
        P("rep", "own", None, None),
        P("own", None, None),
        P("own"),
        P(),
        P(),
        P(),
        P(),
        P("rep", None, None),
        P(),
    )
    return jax.shard_map(
        local,
        mesh=mesh,
        in_specs=placed,
        out_specs=(P("rep", "own", None, None), P("own", None, None), P()),
        check_vma=False,
    )
```

```python
import jax
import jax.numpy as jnp
from jax import lax
from jax.sharding import PartitionSpec as P

TOP_PRECISION = lax.Precision.HIGHEST


def _bits(n):
    return (n - 1).bit_length()


def _pair_perm(n, j):
    return [(i, i ^ (1 << j)) for i in range(n)]


def swap_sum(x, axis):
    n = lax.axis_size(axis)
    for j in range(_bits(n)):
        x = x + lax.ppermute(x, axis, _pair_perm(n, j))
    return x


def _split_plan(shape, steps):
    dims = list(shape)
    plan = []
    for _ in range(steps):
        if dims[-1] > 128:
            axis = len(dims) - 1
        elif dims[-2] > 8:
            axis = len(dims) - 2
        elif dims[-1] % 2 == 0 and dims[-1] >= dims[-2]:
            axis = len(dims) - 1
        else:
            axis = len(dims) - 2
        assert dims[axis] % 2 == 0
        dims[axis] //= 2
        plan.append(axis)
    return plan


def _scalar_rows(rows, count):
    width = max(1, (count - 1).bit_length())
    n = rows.shape[0]
    if n * width > 31:
        return [rows[i] for i in range(n)]
    fields = jnp.left_shift(rows, jnp.arange(n, dtype=rows.dtype) * width)
    packed = jnp.sum(fields)
    return [(packed >> (i * width)) & ((1 << width) - 1) for i in range(n)]


def _pick_rows(table, rows):
    return jnp.stack([lax.dynamic_index_in_dim(table, r, 0, keepdims=False) for r in rows])


def _scatter_rows(parts, rows, count):
    table = jnp.zeros((count,) + parts.shape[1:], parts.dtype)
    for i, r in enumerate(rows):
        slab = lax.dynamic_index_in_dim(table, r, 0, keepdims=True)
        table = lax.dynamic_update_index_in_dim(table, slab + parts[i : i + 1], r, 0)
    return table


def table_rows(x, rows, n_rep, n_own):
    axes = ("rep", "own")
    count = n_rep * n_own
    index = lax.axis_index("rep") * n_own + lax.axis_index("own")
    core = index & 1
    own_bits = _bits(n_own)
    rest = list(range(1, own_bits)) + [own_bits + j for j in range(_bits(n_rep))]
    alt = list(rest)
    for i in range(0, len(alt) - 1, 2):
        alt[i], alt[i + 1] = alt[i + 1], alt[i]
    stages = [(0, 0)] + list(zip(rest, alt))
    tail = min(2, len(rest))
    halving = stages[: len(stages) - tail]
    pairing = stages[len(stages) - tail :]

    def perm_of(p0, p1):
        return [(i, i ^ (1 << (p0 if i % 2 == 0 else p1))) for i in range(count)]

    def bit_of(p0, p1):
        return (index >> jnp.where(core == 0, p0, p1)) & 1

    plan = _split_plan(x.shape, len(halving))
    bits = []
    cur = x
    for (p0, p1), axis in zip(halving, plan):
        bit = bit_of(p0, p1)
        half = cur.shape[axis] // 2
        keep = lax.dynamic_slice_in_dim(cur, bit * half, half, axis)
        send = lax.dynamic_slice_in_dim(cur, (1 - bit) * half, half, axis)
        cur = keep + lax.ppermute(send, axes, perm_of(p0, p1))
        bits.append(bit)
    if len(pairing) == 2:
        (a0, a1), (b0, b1) = pairing

        def group_perm(k):
            pairs = []
            for i in range(count):
                pa, pb = (a0, b0) if i % 2 == 0 else (a1, b1)
                pairs.append((i, i ^ (((k & 1) << pa) | ((k >> 1) << pb))))
            return pairs

        place = bit_of(a0, a1) + 2 * bit_of(b0, b1)
        held = [cur] + [lax.ppermute(cur, axes, group_perm(k)) for k in (1, 2, 3)]
        total = None
        for member in range(4):
            term = lax.select_n(place ^ member, *held)
            total = term if total is None else total + term
        cur = total
    else:
        for p0, p1 in pairing:
            cur = cur + lax.ppermute(cur, axes, perm_of(p0, p1))
    steps_back = list(reversed(list(zip(halving, plan, bits))))
    for index_step, ((p0, p1), axis, bit) in enumerate(steps_back):
        other = lax.ppermute(cur, axes, perm_of(p0, p1))
        if index_step == len(steps_back) - 1:
            cur = _pick_rows(cur, rows)
            other = _pick_rows(other, rows)
        low = jnp.where(bit == 0, cur, other)
        high = jnp.where(bit == 0, other, cur)
        cur = jnp.concatenate([low, high], axis=axis)
    if not steps_back:
        cur = _pick_rows(cur, rows)
    return cur


def local(
    gradient,
    feedback,
    momentum,
    tile_matrix,
    matrix_group,
    group_scale,
    start_basis,
    inverse_gram_factors,
    vector_grad,
    vector_momentum,
):
    replicas = lax.axis_size("rep")
    n_own = lax.axis_size("own")
    matrix_count = start_basis.shape[0]
    selector = (tile_matrix[:, None] == jnp.arange(matrix_count, dtype=jnp.int32)[None, :]).astype(
        jnp.float32
    )
    combined = gradient[0].astype(jnp.float32) + feedback[0]
    tile_rows = _scalar_rows(tile_matrix, matrix_count)
    q_tiles = _pick_rows(start_basis, tile_rows)
    first_local = jnp.einsum("tkd,tds->tks", combined, q_tiles, precision=TOP_PRECISION)
    left_size = first_local.size
    carried = jnp.concatenate([first_local.reshape(-1), vector_grad[0].reshape(-1)])
    carried = swap_sum(carried, "rep")
    first_left = carried[:left_size].reshape(first_local.shape) / replicas
    vector_summed = carried[left_size:].reshape(vector_grad.shape[1:])
    mix_first = _pick_rows(inverse_gram_factors[0], tile_rows)
    mix_right = _pick_rows(inverse_gram_factors[1], tile_rows)
    mix_second = _pick_rows(inverse_gram_factors[2], tile_rows)
    new_vector_momentum = 0.9 * vector_momentum + vector_summed / replicas
    group_select = (
        matrix_group[:, None] == jnp.arange(group_scale.shape[0], dtype=jnp.int32)[None, :]
    ).astype(jnp.float32)
    matrix_scale = jnp.dot(group_select, group_scale, precision=TOP_PRECISION)
    tile_scale = jnp.dot(selector, matrix_scale, precision=TOP_PRECISION)
    first_left, mix_right, mix_second, new_vector_momentum, tile_scale = lax.optimization_barrier(
        (first_left, mix_right, mix_second, new_vector_momentum, tile_scale)
    )
    first_ortho = jnp.einsum("tks,tsa->tka", first_left, mix_first, precision=TOP_PRECISION)
    first_parts = jnp.einsum("tkd,tks->tsd", combined, first_ortho, precision=TOP_PRECISION)
    first_table = _scatter_rows(first_parts, tile_rows, matrix_count)
    first_rows = table_rows(first_table, tile_rows, replicas, n_own) / replicas
    right_rows = jnp.einsum("tjw,tjd->twd", mix_right, first_rows, precision=TOP_PRECISION)
    second_local = jnp.einsum("tkd,tsd->tks", combined, right_rows, precision=TOP_PRECISION)
    second_left = swap_sum(second_local, "rep") / replicas
    second_ortho = jnp.einsum("tks,tsa->tka", second_left, mix_second, precision=TOP_PRECISION)
    second_parts = jnp.einsum("tkd,tks->tsd", combined, second_ortho, precision=TOP_PRECISION)
    second_table = _scatter_rows(second_parts, tile_rows, matrix_count)
    back_rows = table_rows(second_table, tile_rows, replicas, n_own) / replicas
    approximation = jnp.einsum("tks,tsd->tkd", second_ortho, back_rows, precision=TOP_PRECISION)
    new_feedback = (combined - approximation)[None]
    new_momentum = 0.9 * momentum + tile_scale[:, None, None] * approximation
    return (new_feedback, new_momentum, new_vector_momentum)


def solution(mesh):
    placed = (
        P("rep", "own", None, None),
        P("rep", "own", None, None),
        P("own", None, None),
        P("own"),
        P(),
        P(),
        P(),
        P(),
        P("rep", None, None),
        P(),
    )
    return jax.shard_map(
        local,
        mesh=mesh,
        in_specs=placed,
        out_specs=(P("rep", "own", None, None), P("own", None, None), P()),
        check_vma=False,
    )
```

```python
import jax
import jax.numpy as jnp
from jax import lax
from jax.experimental import pallas as pl
from jax.experimental.pallas import tpu as pltpu
from jax.sharding import PartitionSpec as P

TOP_PRECISION = lax.Precision.HIGHEST
WIDE_PRECISION = lax.Precision.HIGH


def _bits(n):
    return (n - 1).bit_length()


def _pair_perm(n, j):
    return [(i, i ^ (1 << j)) for i in range(n)]


def swap_sum(x, axis):
    n = lax.axis_size(axis)
    for j in range(_bits(n)):
        x = x + lax.ppermute(x, axis, _pair_perm(n, j))
    return x


def _split_plan(shape, steps):
    dims = list(shape)
    plan = []
    for _ in range(steps):
        if dims[-1] > 128:
            axis = len(dims) - 1
        elif dims[-2] > 8:
            axis = len(dims) - 2
        elif dims[-1] % 2 == 0 and dims[-1] >= dims[-2]:
            axis = len(dims) - 1
        else:
            axis = len(dims) - 2
        assert dims[axis] % 2 == 0
        dims[axis] //= 2
        plan.append(axis)
    return plan


def _first_kernel(rows_ref, grad_ref, feed_ref, basis_ref, out_ref):
    summed = grad_ref[0, 0].astype(jnp.float32) + feed_ref[0, 0]
    out_ref[0] = lax.dot_general(
        summed,
        basis_ref[0],
        (((1,), (1,)), ((), ())),
        precision=TOP_PRECISION,
        preferred_element_type=jnp.float32,
    )


def first_products(tile_matrix, gradient, feedback, basis_rows):
    tiles, rows, width = gradient.shape[1:]
    rank = basis_rows.shape[1]
    grid_spec = pltpu.PrefetchScalarGridSpec(
        num_scalar_prefetch=1,
        grid=(tiles,),
        in_specs=[
            pl.BlockSpec((1, 1, rows, width), lambda t, idx: (0, t, 0, 0)),
            pl.BlockSpec((1, 1, rows, width), lambda t, idx: (0, t, 0, 0)),
            pl.BlockSpec((1, rank, width), lambda t, idx: (idx[t], 0, 0)),
        ],
        out_specs=pl.BlockSpec((1, rows, rank), lambda t, idx: (t, 0, 0)),
    )
    return pl.pallas_call(
        _first_kernel,
        grid_spec=grid_spec,
        out_shape=jax.ShapeDtypeStruct((tiles, rows, rank), jnp.float32),
        cost_estimate=pl.CostEstimate(
            flops=2 * tiles * rows * width * rank,
            transcendentals=0,
            bytes_accessed=tiles * (rows * width * 6 + rank * width * 4 + rows * rank * 4),
        ),
    )(tile_matrix, gradient, feedback, basis_rows)


def _scalar_rows(rows, count):
    width = max(1, (count - 1).bit_length())
    n = rows.shape[0]
    if n * width > 31:
        return [rows[i] for i in range(n)]
    fields = jnp.left_shift(rows, jnp.arange(n, dtype=rows.dtype) * width)
    packed = jnp.sum(fields)
    return [(packed >> (i * width)) & ((1 << width) - 1) for i in range(n)]


def _pick_rows(table, rows):
    return jnp.stack([lax.dynamic_index_in_dim(table, r, 0, keepdims=False) for r in rows])


def _scatter_rows(parts, rows, count):
    table = jnp.zeros((count,) + parts.shape[1:], parts.dtype)
    for i, r in enumerate(rows):
        slab = lax.dynamic_index_in_dim(table, r, 0, keepdims=True)
        table = lax.dynamic_update_index_in_dim(table, slab + parts[i : i + 1], r, 0)
    return table


def table_rows(x, rows, n_rep, n_own):
    axes = ("rep", "own")
    count = n_rep * n_own
    index = lax.axis_index("rep") * n_own + lax.axis_index("own")
    core = index & 1
    own_bits = _bits(n_own)
    rest = list(range(1, own_bits)) + [own_bits + j for j in range(_bits(n_rep))]
    alt = list(rest)
    for i in range(0, len(alt) - 1, 2):
        alt[i], alt[i + 1] = alt[i + 1], alt[i]
    stages = [(0, 0)] + list(zip(rest, alt))
    tail = min(2, len(rest))
    halving = stages[: len(stages) - tail]
    pairing = stages[len(stages) - tail :]

    def perm_of(p0, p1):
        return [(i, i ^ (1 << (p0 if i % 2 == 0 else p1))) for i in range(count)]

    def bit_of(p0, p1):
        return (index >> jnp.where(core == 0, p0, p1)) & 1

    plan = _split_plan(x.shape, len(halving))
    bits = []
    cur = x
    for (p0, p1), axis in zip(halving, plan):
        bit = bit_of(p0, p1)
        half = cur.shape[axis] // 2
        keep = lax.dynamic_slice_in_dim(cur, bit * half, half, axis)
        send = lax.dynamic_slice_in_dim(cur, (1 - bit) * half, half, axis)
        cur = keep + lax.ppermute(send, axes, perm_of(p0, p1))
        bits.append(bit)
    if len(pairing) == 2:
        (a0, a1), (b0, b1) = pairing

        def group_perm(k):
            pairs = []
            for i in range(count):
                pa, pb = (a0, b0) if i % 2 == 0 else (a1, b1)
                pairs.append((i, i ^ (((k & 1) << pa) | ((k >> 1) << pb))))
            return pairs

        place = bit_of(a0, a1) + 2 * bit_of(b0, b1)
        held = [cur] + [lax.ppermute(cur, axes, group_perm(k)) for k in (1, 2, 3)]
        total = None
        for member in range(4):
            term = lax.select_n(place ^ member, *held)
            total = term if total is None else total + term
        cur = total
    else:
        for p0, p1 in pairing:
            cur = cur + lax.ppermute(cur, axes, perm_of(p0, p1))
    steps_back = list(reversed(list(zip(halving, plan, bits))))
    for index_step, ((p0, p1), axis, bit) in enumerate(steps_back):
        other = lax.ppermute(cur, axes, perm_of(p0, p1))
        if index_step == len(steps_back) - 1:
            cur = _pick_rows(cur, rows)
            other = _pick_rows(other, rows)
        low = jnp.where(bit == 0, cur, other)
        high = jnp.where(bit == 0, other, cur)
        cur = jnp.concatenate([low, high], axis=axis)
    if not steps_back:
        cur = _pick_rows(cur, rows)
    return cur


def local(
    gradient,
    feedback,
    momentum,
    tile_matrix,
    matrix_group,
    group_scale,
    start_basis,
    inverse_gram_factors,
    vector_grad,
    vector_momentum,
):
    replicas = lax.axis_size("rep")
    n_own = lax.axis_size("own")
    matrix_count = start_basis.shape[0]
    selector = (tile_matrix[:, None] == jnp.arange(matrix_count, dtype=jnp.int32)[None, :]).astype(
        jnp.float32
    )
    combined = gradient[0].astype(jnp.float32) + feedback[0]
    tile_rows = _scalar_rows(tile_matrix, matrix_count)
    first_local = first_products(tile_matrix, gradient, feedback, jnp.swapaxes(start_basis, 1, 2))
    left_size = first_local.size
    carried = jnp.concatenate([first_local.reshape(-1), vector_grad[0].reshape(-1)])
    carried = swap_sum(carried, "rep")
    first_left = carried[:left_size].reshape(first_local.shape) / replicas
    vector_summed = carried[left_size:].reshape(vector_grad.shape[1:])
    mix_first = _pick_rows(inverse_gram_factors[0], tile_rows)
    mix_right = _pick_rows(inverse_gram_factors[1], tile_rows)
    mix_second = _pick_rows(inverse_gram_factors[2], tile_rows)
    new_vector_momentum = 0.9 * vector_momentum + vector_summed / replicas
    group_select = (
        matrix_group[:, None] == jnp.arange(group_scale.shape[0], dtype=jnp.int32)[None, :]
    ).astype(jnp.float32)
    matrix_scale = jnp.dot(group_select, group_scale, precision=TOP_PRECISION)
    tile_scale = jnp.dot(selector, matrix_scale, precision=TOP_PRECISION)
    first_left, mix_right, mix_second, new_vector_momentum, tile_scale = lax.optimization_barrier(
        (first_left, mix_right, mix_second, new_vector_momentum, tile_scale)
    )
    first_ortho = jnp.einsum("tks,tsa->tka", first_left, mix_first, precision=TOP_PRECISION)
    first_parts = jnp.einsum("tkd,tks->tsd", combined, first_ortho, precision=WIDE_PRECISION)
    first_table = _scatter_rows(first_parts, tile_rows, matrix_count)
    first_rows = table_rows(first_table, tile_rows, replicas, n_own) / replicas
    right_rows = jnp.einsum("tjw,tjd->twd", mix_right, first_rows, precision=TOP_PRECISION)
    second_local = jnp.einsum("tkd,tsd->tks", combined, right_rows, precision=WIDE_PRECISION)
    second_left = swap_sum(second_local, "rep") / replicas
    second_ortho = jnp.einsum("tks,tsa->tka", second_left, mix_second, precision=TOP_PRECISION)
    second_parts = jnp.einsum("tkd,tks->tsd", combined, second_ortho, precision=WIDE_PRECISION)
    second_table = _scatter_rows(second_parts, tile_rows, matrix_count)
    back_rows = table_rows(second_table, tile_rows, replicas, n_own) / replicas
    approximation = jnp.einsum("tks,tsd->tkd", second_ortho, back_rows, precision=WIDE_PRECISION)
    new_feedback = (combined - approximation)[None]
    new_momentum = 0.9 * momentum + tile_scale[:, None, None] * approximation
    return (new_feedback, new_momentum, new_vector_momentum)


def solution(mesh):
    placed = (
        P("rep", "own", None, None),
        P("rep", "own", None, None),
        P("own", None, None),
        P("own"),
        P(),
        P(),
        P(),
        P(),
        P("rep", None, None),
        P(),
    )
    return jax.shard_map(
        local,
        mesh=mesh,
        in_specs=placed,
        out_specs=(P("rep", "own", None, None), P("own", None, None), P()),
        check_vma=False,
    )
```

```python
import jax
import jax.numpy as jnp
from jax import lax
from jax.experimental import pallas as pl
from jax.experimental.pallas import tpu as pltpu
from jax.sharding import PartitionSpec as P

TOP_PRECISION = lax.Precision.HIGHEST
WIDE_PRECISION = lax.Precision.HIGH


def _bits(n):
    return (n - 1).bit_length()


def _pair_perm(n, j):
    return [(i, i ^ (1 << j)) for i in range(n)]


def swap_sum(x, axis):
    n = lax.axis_size(axis)
    for j in range(_bits(n)):
        x = x + lax.ppermute(x, axis, _pair_perm(n, j))
    return x


def _split_plan(shape, steps):
    dims = list(shape)
    plan = []
    for _ in range(steps):
        if dims[-1] > 128:
            axis = len(dims) - 1
        elif dims[-2] > 8:
            axis = len(dims) - 2
        elif dims[-1] % 2 == 0 and dims[-1] >= dims[-2]:
            axis = len(dims) - 1
        else:
            axis = len(dims) - 2
        assert dims[axis] % 2 == 0
        dims[axis] //= 2
        plan.append(axis)
    return plan


def _first_kernel(rows_ref, grad_ref, feed_ref, basis_ref, out_ref):
    summed = grad_ref[0, 0].astype(jnp.float32) + feed_ref[0, 0]
    basis = basis_ref[0]
    summed_hi = summed.astype(jnp.bfloat16)
    summed_lo = (summed - summed_hi.astype(jnp.float32)).astype(jnp.bfloat16)
    basis_hi = basis.astype(jnp.bfloat16)
    basis_lo = (basis - basis_hi.astype(jnp.float32)).astype(jnp.bfloat16)

    def product(a, b):
        return lax.dot_general(a, b, (((1,), (1,)), ((), ())), preferred_element_type=jnp.float32)

    out_ref[0] = product(summed_hi, basis_hi) + (product(summed_hi, basis_lo) + product(summed_lo, basis_hi))


def first_products(tile_matrix, gradient, feedback, basis_rows):
    tiles, rows, width = gradient.shape[1:]
    rank = basis_rows.shape[1]
    grid_spec = pltpu.PrefetchScalarGridSpec(
        num_scalar_prefetch=1,
        grid=(tiles,),
        in_specs=[
            pl.BlockSpec((1, 1, rows, width), lambda t, idx: (0, t, 0, 0)),
            pl.BlockSpec((1, 1, rows, width), lambda t, idx: (0, t, 0, 0)),
            pl.BlockSpec((1, rank, width), lambda t, idx: (idx[t], 0, 0)),
        ],
        out_specs=pl.BlockSpec((1, rows, rank), lambda t, idx: (t, 0, 0)),
    )
    return pl.pallas_call(
        _first_kernel,
        grid_spec=grid_spec,
        out_shape=jax.ShapeDtypeStruct((tiles, rows, rank), jnp.float32),
        cost_estimate=pl.CostEstimate(
            flops=2 * tiles * rows * width * rank,
            transcendentals=0,
            bytes_accessed=tiles * (rows * width * 6 + rank * width * 4 + rows * rank * 4),
        ),
    )(tile_matrix, gradient, feedback, basis_rows)


def _scalar_rows(rows, count):
    width = max(1, (count - 1).bit_length())
    n = rows.shape[0]
    if n * width > 31:
        return [rows[i] for i in range(n)]
    fields = jnp.left_shift(rows, jnp.arange(n, dtype=rows.dtype) * width)
    packed = jnp.sum(fields)
    return [(packed >> (i * width)) & ((1 << width) - 1) for i in range(n)]


def _pick_rows(table, rows):
    return jnp.stack([lax.dynamic_index_in_dim(table, r, 0, keepdims=False) for r in rows])


def _scatter_rows(parts, rows, count):
    table = jnp.zeros((count,) + parts.shape[1:], parts.dtype)
    for i, r in enumerate(rows):
        slab = lax.dynamic_index_in_dim(table, r, 0, keepdims=True)
        table = lax.dynamic_update_index_in_dim(table, slab + parts[i : i + 1], r, 0)
    return table


def table_rows(x, rows, n_rep, n_own):
    axes = ("rep", "own")
    count = n_rep * n_own
    index = lax.axis_index("rep") * n_own + lax.axis_index("own")
    core = index & 1
    own_bits = _bits(n_own)
    rest = list(range(1, own_bits)) + [own_bits + j for j in range(_bits(n_rep))]
    alt = list(rest)
    for i in range(0, len(alt) - 1, 2):
        alt[i], alt[i + 1] = alt[i + 1], alt[i]
    stages = [(0, 0)] + list(zip(rest, alt))
    tail = min(2, len(rest))
    halving = stages[: len(stages) - tail]
    pairing = stages[len(stages) - tail :]

    def perm_of(p0, p1):
        return [(i, i ^ (1 << (p0 if i % 2 == 0 else p1))) for i in range(count)]

    def bit_of(p0, p1):
        return (index >> jnp.where(core == 0, p0, p1)) & 1

    plan = _split_plan(x.shape, len(halving))
    bits = []
    cur = x
    for (p0, p1), axis in zip(halving, plan):
        bit = bit_of(p0, p1)
        half = cur.shape[axis] // 2
        keep = lax.dynamic_slice_in_dim(cur, bit * half, half, axis)
        send = lax.dynamic_slice_in_dim(cur, (1 - bit) * half, half, axis)
        cur = keep + lax.ppermute(send, axes, perm_of(p0, p1))
        bits.append(bit)
    if len(pairing) == 2:
        (a0, a1), (b0, b1) = pairing

        def group_perm(k):
            pairs = []
            for i in range(count):
                pa, pb = (a0, b0) if i % 2 == 0 else (a1, b1)
                pairs.append((i, i ^ (((k & 1) << pa) | ((k >> 1) << pb))))
            return pairs

        place = bit_of(a0, a1) + 2 * bit_of(b0, b1)
        held = [cur] + [lax.ppermute(cur, axes, group_perm(k)) for k in (1, 2, 3)]
        total = None
        for member in range(4):
            term = lax.select_n(place ^ member, *held)
            total = term if total is None else total + term
        cur = total
    else:
        for p0, p1 in pairing:
            cur = cur + lax.ppermute(cur, axes, perm_of(p0, p1))
    steps_back = list(reversed(list(zip(halving, plan, bits))))
    for index_step, ((p0, p1), axis, bit) in enumerate(steps_back):
        other = lax.ppermute(cur, axes, perm_of(p0, p1))
        if index_step == len(steps_back) - 1:
            cur = _pick_rows(cur, rows)
            other = _pick_rows(other, rows)
        low = jnp.where(bit == 0, cur, other)
        high = jnp.where(bit == 0, other, cur)
        cur = jnp.concatenate([low, high], axis=axis)
    if not steps_back:
        cur = _pick_rows(cur, rows)
    return cur


def local(
    gradient,
    feedback,
    momentum,
    tile_matrix,
    matrix_group,
    group_scale,
    start_basis,
    inverse_gram_factors,
    vector_grad,
    vector_momentum,
):
    replicas = lax.axis_size("rep")
    n_own = lax.axis_size("own")
    matrix_count = start_basis.shape[0]
    selector = (tile_matrix[:, None] == jnp.arange(matrix_count, dtype=jnp.int32)[None, :]).astype(
        jnp.float32
    )
    combined = gradient[0].astype(jnp.float32) + feedback[0]
    tile_rows = _scalar_rows(tile_matrix, matrix_count)
    first_local = first_products(tile_matrix, gradient, feedback, jnp.swapaxes(start_basis, 1, 2))
    left_size = first_local.size
    carried = jnp.concatenate([first_local.reshape(-1), vector_grad[0].reshape(-1)])
    carried = swap_sum(carried, "rep")
    first_left = carried[:left_size].reshape(first_local.shape) / replicas
    vector_summed = carried[left_size:].reshape(vector_grad.shape[1:])
    mix_first = _pick_rows(inverse_gram_factors[0], tile_rows)
    mix_right = _pick_rows(inverse_gram_factors[1], tile_rows)
    mix_second = _pick_rows(inverse_gram_factors[2], tile_rows)
    new_vector_momentum = 0.9 * vector_momentum + vector_summed / replicas
    group_select = (
        matrix_group[:, None] == jnp.arange(group_scale.shape[0], dtype=jnp.int32)[None, :]
    ).astype(jnp.float32)
    matrix_scale = jnp.dot(group_select, group_scale, precision=TOP_PRECISION)
    tile_scale = jnp.dot(selector, matrix_scale, precision=TOP_PRECISION)
    first_left, mix_right, mix_second, new_vector_momentum, tile_scale = lax.optimization_barrier(
        (first_left, mix_right, mix_second, new_vector_momentum, tile_scale)
    )
    first_ortho = jnp.einsum("tks,tsa->tka", first_left, mix_first, precision=TOP_PRECISION)
    first_parts = jnp.einsum("tkd,tks->tsd", combined, first_ortho, precision=WIDE_PRECISION)
    first_table = _scatter_rows(first_parts, tile_rows, matrix_count)
    first_rows = table_rows(first_table, tile_rows, replicas, n_own) / replicas
    right_rows = jnp.einsum("tjw,tjd->twd", mix_right, first_rows, precision=TOP_PRECISION)
    second_local = jnp.einsum("tkd,tsd->tks", combined, right_rows, precision=WIDE_PRECISION)
    second_left = swap_sum(second_local, "rep") / replicas
    second_ortho = jnp.einsum("tks,tsa->tka", second_left, mix_second, precision=TOP_PRECISION)
    second_parts = jnp.einsum("tkd,tks->tsd", combined, second_ortho, precision=WIDE_PRECISION)
    second_table = _scatter_rows(second_parts, tile_rows, matrix_count)
    back_rows = table_rows(second_table, tile_rows, replicas, n_own) / replicas
    approximation = jnp.einsum("tks,tsd->tkd", second_ortho, back_rows, precision=WIDE_PRECISION)
    new_feedback = (combined - approximation)[None]
    new_momentum = 0.9 * momentum + tile_scale[:, None, None] * approximation
    return (new_feedback, new_momentum, new_vector_momentum)


def solution(mesh):
    placed = (
        P("rep", "own", None, None),
        P("rep", "own", None, None),
        P("own", None, None),
        P("own"),
        P(),
        P(),
        P(),
        P(),
        P("rep", None, None),
        P(),
    )
    return jax.shard_map(
        local,
        mesh=mesh,
        in_specs=placed,
        out_specs=(P("rep", "own", None, None), P("own", None, None), P()),
        check_vma=False,
    )
```

```python
import jax
import jax.numpy as jnp
from jax import lax
from jax.sharding import PartitionSpec as P

TOP_PRECISION = lax.Precision.HIGHEST
WIDE_PRECISION = lax.Precision.HIGH


def _bits(n):
    return (n - 1).bit_length()


def _pair_perm(n, j):
    return [(i, i ^ (1 << j)) for i in range(n)]


def swap_sum(x, axis):
    n = lax.axis_size(axis)
    for j in range(_bits(n)):
        x = x + lax.ppermute(x, axis, _pair_perm(n, j))
    return x


def _split_plan(shape, steps):
    dims = list(shape)
    plan = []
    for _ in range(steps):
        if dims[-1] > 128:
            axis = len(dims) - 1
        elif dims[-2] > 8:
            axis = len(dims) - 2
        elif dims[-1] % 2 == 0 and dims[-1] >= dims[-2]:
            axis = len(dims) - 1
        else:
            axis = len(dims) - 2
        assert dims[axis] % 2 == 0
        dims[axis] //= 2
        plan.append(axis)
    return plan


def _scalar_rows(rows, count):
    width = max(1, (count - 1).bit_length())
    n = rows.shape[0]
    if n * width > 31:
        return [rows[i] for i in range(n)]
    fields = jnp.left_shift(rows, jnp.arange(n, dtype=rows.dtype) * width)
    packed = jnp.sum(fields)
    return [(packed >> (i * width)) & ((1 << width) - 1) for i in range(n)]


def _pick_rows(table, rows):
    return jnp.stack([lax.dynamic_index_in_dim(table, r, 0, keepdims=False) for r in rows])


def _scatter_rows(parts, rows, count):
    table = jnp.zeros((count,) + parts.shape[1:], parts.dtype)
    for i, r in enumerate(rows):
        slab = lax.dynamic_index_in_dim(table, r, 0, keepdims=True)
        table = lax.dynamic_update_index_in_dim(table, slab + parts[i : i + 1], r, 0)
    return table


def table_rows(x, rows, n_rep, n_own):
    axes = ("rep", "own")
    count = n_rep * n_own
    index = lax.axis_index("rep") * n_own + lax.axis_index("own")
    core = index & 1
    own_bits = _bits(n_own)
    rest = list(range(1, own_bits)) + [own_bits + j for j in range(_bits(n_rep))]
    alt = list(rest)
    for i in range(0, len(alt) - 1, 2):
        alt[i], alt[i + 1] = alt[i + 1], alt[i]
    stages = [(0, 0)] + list(zip(rest, alt))
    tail = min(2, len(rest))
    halving = stages[: len(stages) - tail]
    pairing = stages[len(stages) - tail :]

    def perm_of(p0, p1):
        return [(i, i ^ (1 << (p0 if i % 2 == 0 else p1))) for i in range(count)]

    def bit_of(p0, p1):
        return (index >> jnp.where(core == 0, p0, p1)) & 1

    plan = _split_plan(x.shape, len(halving))
    bits = []
    cur = x
    for (p0, p1), axis in zip(halving, plan):
        bit = bit_of(p0, p1)
        half = cur.shape[axis] // 2
        keep = lax.dynamic_slice_in_dim(cur, bit * half, half, axis)
        send = lax.dynamic_slice_in_dim(cur, (1 - bit) * half, half, axis)
        cur = keep + lax.ppermute(send, axes, perm_of(p0, p1))
        bits.append(bit)
    if len(pairing) == 2:
        (a0, a1), (b0, b1) = pairing

        def group_perm(k):
            pairs = []
            for i in range(count):
                pa, pb = (a0, b0) if i % 2 == 0 else (a1, b1)
                pairs.append((i, i ^ (((k & 1) << pa) | ((k >> 1) << pb))))
            return pairs

        place = bit_of(a0, a1) + 2 * bit_of(b0, b1)
        diagonal = lax.ppermute(cur, axes, group_perm(3))
        sides = [lax.ppermute(cur, axes, group_perm(k)) for k in (1, 2)]
        held = [cur] + sides + [diagonal]
        total = None
        for member in range(4):
            term = lax.select_n(place ^ member, *held)
            total = term if total is None else total + term
        cur = total
    else:
        for p0, p1 in pairing:
            cur = cur + lax.ppermute(cur, axes, perm_of(p0, p1))
    steps_back = list(reversed(list(zip(halving, plan, bits))))
    for index_step, ((p0, p1), axis, bit) in enumerate(steps_back):
        other = lax.ppermute(cur, axes, perm_of(p0, p1))
        if index_step == len(steps_back) - 1:
            cur = _pick_rows(cur, rows)
            other = _pick_rows(other, rows)
        low = jnp.where(bit == 0, cur, other)
        high = jnp.where(bit == 0, other, cur)
        cur = jnp.concatenate([low, high], axis=axis)
    if not steps_back:
        cur = _pick_rows(cur, rows)
    return cur


def local(
    gradient,
    feedback,
    momentum,
    tile_matrix,
    matrix_group,
    group_scale,
    start_basis,
    inverse_gram_factors,
    vector_grad,
    vector_momentum,
):
    replicas = lax.axis_size("rep")
    n_own = lax.axis_size("own")
    matrix_count = start_basis.shape[0]
    selector = (tile_matrix[:, None] == jnp.arange(matrix_count, dtype=jnp.int32)[None, :]).astype(
        jnp.float32
    )
    combined = gradient[0].astype(jnp.float32) + feedback[0]
    tile_rows = _scalar_rows(tile_matrix, matrix_count)
    q_tiles = _pick_rows(start_basis, tile_rows)
    first_local = jnp.einsum("tkd,tds->tks", combined, q_tiles, precision=WIDE_PRECISION)
    vector_summed = swap_sum(vector_grad[0], "rep")
    first_left = swap_sum(first_local, "rep") / replicas
    mix_first = _pick_rows(inverse_gram_factors[0], tile_rows)
    mix_right = _pick_rows(inverse_gram_factors[1], tile_rows)
    mix_second = _pick_rows(inverse_gram_factors[2], tile_rows)
    new_vector_momentum = 0.9 * vector_momentum + vector_summed / replicas
    group_select = (
        matrix_group[:, None] == jnp.arange(group_scale.shape[0], dtype=jnp.int32)[None, :]
    ).astype(jnp.float32)
    matrix_scale = jnp.dot(group_select, group_scale, precision=TOP_PRECISION)
    tile_scale = jnp.dot(selector, matrix_scale, precision=TOP_PRECISION)
    first_left, mix_right, mix_second, new_vector_momentum, tile_scale = lax.optimization_barrier(
        (first_left, mix_right, mix_second, new_vector_momentum, tile_scale)
    )
    first_ortho = jnp.einsum("tks,tsa->tka", first_left, mix_first, precision=TOP_PRECISION)
    first_parts = jnp.einsum("tkd,tks->tsd", combined, first_ortho, precision=WIDE_PRECISION)
    first_table = _scatter_rows(first_parts, tile_rows, matrix_count)
    first_rows = table_rows(first_table, tile_rows, replicas, n_own) / replicas
    right_rows = jnp.einsum("tjw,tjd->twd", mix_right, first_rows, precision=TOP_PRECISION)
    second_local = jnp.einsum("tkd,tsd->tks", combined, right_rows, precision=WIDE_PRECISION)
    second_left = swap_sum(second_local, "rep") / replicas
    second_ortho = jnp.einsum("tks,tsa->tka", second_left, mix_second, precision=TOP_PRECISION)
    second_parts = jnp.einsum("tkd,tks->tsd", combined, second_ortho, precision=WIDE_PRECISION)
    second_table = _scatter_rows(second_parts, tile_rows, matrix_count)
    back_rows = table_rows(second_table, tile_rows, replicas, n_own) / replicas
    approximation = jnp.einsum("tks,tsd->tkd", second_ortho, back_rows, precision=WIDE_PRECISION)
    new_feedback = (combined - approximation)[None]
    new_momentum = 0.9 * momentum + tile_scale[:, None, None] * approximation
    return (new_feedback, new_momentum, new_vector_momentum)


def solution(mesh):
    placed = (
        P("rep", "own", None, None),
        P("rep", "own", None, None),
        P("own", None, None),
        P("own"),
        P(),
        P(),
        P(),
        P(),
        P("rep", None, None),
        P(),
    )
    return jax.shard_map(
        local,
        mesh=mesh,
        in_specs=placed,
        out_specs=(P("rep", "own", None, None), P("own", None, None), P()),
        check_vma=False,
    )
```

```python
import jax
import jax.numpy as jnp
from jax import lax
from jax.sharding import PartitionSpec as P

TOP_PRECISION = lax.Precision.HIGHEST
WIDE_PRECISION = lax.Precision.HIGH


def _bits(n):
    return (n - 1).bit_length()


def _pair_perm(n, j):
    return [(i, i ^ (1 << j)) for i in range(n)]


def swap_sum(x, axis):
    n = lax.axis_size(axis)
    for j in range(_bits(n)):
        x = x + lax.ppermute(x, axis, _pair_perm(n, j))
    return x


def _split_plan(shape, steps):
    dims = list(shape)
    plan = []
    for _ in range(steps):
        if dims[-1] > 128:
            axis = len(dims) - 1
        elif dims[-2] > 8:
            axis = len(dims) - 2
        elif dims[-1] % 2 == 0 and dims[-1] >= dims[-2]:
            axis = len(dims) - 1
        else:
            axis = len(dims) - 2
        assert dims[axis] % 2 == 0
        dims[axis] //= 2
        plan.append(axis)
    return plan


def _scalar_rows(rows, count):
    width = max(1, (count - 1).bit_length())
    n = rows.shape[0]
    if n * width > 31:
        return [rows[i] for i in range(n)]
    fields = jnp.left_shift(rows, jnp.arange(n, dtype=rows.dtype) * width)
    packed = jnp.sum(fields)
    return [(packed >> (i * width)) & ((1 << width) - 1) for i in range(n)]


def _pick_rows(table, rows):
    return jnp.stack([lax.dynamic_index_in_dim(table, r, 0, keepdims=False) for r in rows])


def _scatter_rows(parts, rows, count):
    table = jnp.zeros((count,) + parts.shape[1:], parts.dtype)
    for i, r in enumerate(rows):
        slab = lax.dynamic_index_in_dim(table, r, 0, keepdims=True)
        table = lax.dynamic_update_index_in_dim(table, slab + parts[i : i + 1], r, 0)
    return table


def table_rows(x, rows, n_rep, n_own):
    axes = ("rep", "own")
    count = n_rep * n_own
    index = lax.axis_index("rep") * n_own + lax.axis_index("own")
    core = index & 1
    own_bits = _bits(n_own)
    rest = list(range(1, own_bits)) + [own_bits + j for j in range(_bits(n_rep))]
    alt = list(rest)
    for i in range(0, len(alt) - 1, 2):
        alt[i], alt[i + 1] = alt[i + 1], alt[i]
    stages = [(0, 0)] + list(zip(rest, alt))
    tail = min(2, len(rest))
    halving = stages[: len(stages) - tail]
    pairing = stages[len(stages) - tail :]

    def perm_of(p0, p1):
        return [(i, i ^ (1 << (p0 if i % 2 == 0 else p1))) for i in range(count)]

    def bit_of(p0, p1):
        return (index >> jnp.where(core == 0, p0, p1)) & 1

    plan = _split_plan(x.shape, len(halving))
    bits = []
    cur = x
    for (p0, p1), axis in zip(halving, plan):
        bit = bit_of(p0, p1)
        half = cur.shape[axis] // 2
        keep = lax.dynamic_slice_in_dim(cur, bit * half, half, axis)
        send = lax.dynamic_slice_in_dim(cur, (1 - bit) * half, half, axis)
        cur = keep + lax.ppermute(send, axes, perm_of(p0, p1))
        bits.append(bit)
    if len(pairing) == 2:
        (a0, a1), (b0, b1) = pairing

        def group_perm(k):
            pairs = []
            for i in range(count):
                pa, pb = (a0, b0) if i % 2 == 0 else (a1, b1)
                pairs.append((i, i ^ (((k & 1) << pa) | ((k >> 1) << pb))))
            return pairs

        place = bit_of(a0, a1) + 2 * bit_of(b0, b1)
        diagonal = lax.ppermute(cur, axes, group_perm(3))
        near = lax.ppermute(cur, axes, group_perm(2))
        far = lax.ppermute(cur, axes, group_perm(1))
        sides = [far, near]
        held = [cur] + sides + [diagonal]
        total = None
        for member in range(4):
            term = lax.select_n(place ^ member, *held)
            total = term if total is None else total + term
        cur = total
    else:
        for p0, p1 in pairing:
            cur = cur + lax.ppermute(cur, axes, perm_of(p0, p1))
    steps_back = list(reversed(list(zip(halving, plan, bits))))
    for index_step, ((p0, p1), axis, bit) in enumerate(steps_back):
        other = lax.ppermute(cur, axes, perm_of(p0, p1))
        if index_step == len(steps_back) - 1:
            cur = _pick_rows(cur, rows)
            other = _pick_rows(other, rows)
        low = jnp.where(bit == 0, cur, other)
        high = jnp.where(bit == 0, other, cur)
        cur = jnp.concatenate([low, high], axis=axis)
    if not steps_back:
        cur = _pick_rows(cur, rows)
    return cur


def local(
    gradient,
    feedback,
    momentum,
    tile_matrix,
    matrix_group,
    group_scale,
    start_basis,
    inverse_gram_factors,
    vector_grad,
    vector_momentum,
):
    replicas = lax.axis_size("rep")
    n_own = lax.axis_size("own")
    matrix_count = start_basis.shape[0]
    selector = (tile_matrix[:, None] == jnp.arange(matrix_count, dtype=jnp.int32)[None, :]).astype(
        jnp.float32
    )
    combined = gradient[0].astype(jnp.float32) + feedback[0]
    tile_rows = _scalar_rows(tile_matrix, matrix_count)
    q_tiles = _pick_rows(start_basis, tile_rows)
    first_local = jnp.einsum("tkd,tds->tks", combined, q_tiles, precision=WIDE_PRECISION)
    left_size = first_local.size
    carried = jnp.concatenate([first_local.reshape(-1), vector_grad[0].reshape(-1)])
    carried = swap_sum(carried, "rep")
    first_left = carried[:left_size].reshape(first_local.shape) / replicas
    vector_summed = carried[left_size:].reshape(vector_grad.shape[1:])
    mix_first = _pick_rows(inverse_gram_factors[0], tile_rows)
    mix_right = _pick_rows(inverse_gram_factors[1], tile_rows)
    mix_second = _pick_rows(inverse_gram_factors[2], tile_rows)
    new_vector_momentum = 0.9 * vector_momentum + vector_summed / replicas
    group_select = (
        matrix_group[:, None] == jnp.arange(group_scale.shape[0], dtype=jnp.int32)[None, :]
    ).astype(jnp.float32)
    matrix_scale = jnp.dot(group_select, group_scale, precision=TOP_PRECISION)
    tile_scale = jnp.dot(selector, matrix_scale, precision=TOP_PRECISION)
    first_left, mix_right, mix_second, new_vector_momentum, tile_scale = lax.optimization_barrier(
        (first_left, mix_right, mix_second, new_vector_momentum, tile_scale)
    )
    first_ortho = jnp.einsum("tks,tsa->tka", first_left, mix_first, precision=TOP_PRECISION)
    first_parts = jnp.einsum("tkd,tks->tsd", combined, first_ortho, precision=WIDE_PRECISION)
    first_table = _scatter_rows(first_parts, tile_rows, matrix_count)
    first_rows = table_rows(first_table, tile_rows, replicas, n_own) / replicas
    right_rows = jnp.einsum("tjw,tjd->twd", mix_right, first_rows, precision=TOP_PRECISION)
    second_local = jnp.einsum("tkd,tsd->tks", combined, right_rows, precision=WIDE_PRECISION)
    second_left = swap_sum(second_local, "rep") / replicas
    second_ortho = jnp.einsum("tks,tsa->tka", second_left, mix_second, precision=TOP_PRECISION)
    second_parts = jnp.einsum("tkd,tks->tsd", combined, second_ortho, precision=WIDE_PRECISION)
    second_table = _scatter_rows(second_parts, tile_rows, matrix_count)
    back_rows = table_rows(second_table, tile_rows, replicas, n_own) / replicas
    approximation = jnp.einsum("tks,tsd->tkd", second_ortho, back_rows, precision=WIDE_PRECISION)
    new_feedback = (combined - approximation)[None]
    new_momentum = 0.9 * momentum + tile_scale[:, None, None] * approximation
    return (new_feedback, new_momentum, new_vector_momentum)


def solution(mesh):
    placed = (
        P("rep", "own", None, None),
        P("rep", "own", None, None),
        P("own", None, None),
        P("own"),
        P(),
        P(),
        P(),
        P(),
        P("rep", None, None),
        P(),
    )
    return jax.shard_map(
        local,
        mesh=mesh,
        in_specs=placed,
        out_specs=(P("rep", "own", None, None), P("own", None, None), P()),
        check_vma=False,
    )
```
